512 devices in a mesh: dp: 64 (over z, x, core), mp: 8 (over y).
Axes of the slice: x: 4, y: 8, z: 8, core: 2. Of those that a mesh axis runs over, the one named last changes fastest.
Arguments:
- micro_grads: bfloat16 [64, 2, 768, 768], P('dp', None, None, 'mp'), may hold values from -16 to 16
- master: float32 [768, 768], P('dp', 'mp'), may hold values from -0.21875 to 0.21875
- moment: float32 [768, 768], P('dp', 'mp'), may hold values from -1.5 to 1.5
- second: float32 [768, 768], P('dp', 'mp'), may hold values from 0.001 to 0.1
- left_basis: float32 [768, 768], P(None, 'dp'), may hold values from -0.21875 to 0.21875
- right_basis: float32 [768, 768], P(None, 'mp'), may hold values from -0.21875 to 0.21875
- left_stat: float32 [768, 768], P('mp'), may hold values from -2 to 5, as said below
- right_stat: float32 [768, 768], P('mp'), may hold values from -2 to 5, as said below
Outputs:
- weights_block: bfloat16 [768, 768], P(None, 'mp')
- new_master: float32 [768, 768], P('dp', 'mp')
- new_moment: float32 [768, 768], P('dp', 'mp')
- new_second: float32 [768, 768], P('dp', 'mp')
- new_left_stat: float32 [768, 768], P('mp')
- new_right_stat: float32 [768, 768], P('mp')
- new_left_basis: float32 [768, 768], P('mp')
- new_right_basis: float32 [768, 768], P('mp')
The draws below stay inside these ranges and needn't reach their ends.
Inputs may be any that keep to these rules, and one draw needn't show every extreme that they name: `left_stat`: symmetric. `right_stat`: symmetric.
All inputs are finite; a program needn't handle non-finite values.
Results may differ from the reference program's by a relative error of at most 0.004.
The reference program's roundings to bfloat16 on the way count: a program that leaves them out, or rounds other values in their place, can miss the bound.
Values may be sent and summed in bfloat16 or wider, within the bound.
No kernel may reach another device: no remote copies, remote signals or barrier semaphores. Data moves between devices by JAX's collectives and lax.ppermute only.
A program may use at most 64 MiB of HBM per device.

```python
import math
import jax
import jax.numpy as jnp
from jax import lax

D = 768
MB = 2
N_DP = 64


def stat_matrix(key):
    key_diag, key_noise = jax.random.split(key, 2)
    diagonal = jnp.exp(jax.random.uniform(key_diag, (D,), jnp.float32, 0.0, math.log(3.0)))
    noise = jax.random.normal(key_noise, (D, D), jnp.float32) * 0.08
    symmetric = 0.5 * (noise + noise.T)
    return symmetric + jnp.diag(diagonal)


def draw_left_stat(key, part):
    return stat_matrix(jax.random.fold_in(key, 11))


def draw_right_stat(key, part):
    return stat_matrix(jax.random.fold_in(key, 12))


def strengthened(result, stream_key, source, target, shards_of, factor):
    def block_of(position):
        return (jnp.arange(result.shape[position]) // (result.shape[position] // shards_of)).reshape((-1,) + (1,) * (result.ndim - 1 - position))

    near = jax.random.permutation(stream_key, shards_of)[block_of(target)]
    second = (block_of(target) + shards_of // 2) % shards_of
    return jnp.where((block_of(source) == near) | (block_of(source) == second), factor * result, result)


def block_scale(key, shape, cuts, low, largest):
    gain = 1.0
    for axis_at, parts in cuts:
        heights = jax.random.uniform(jax.random.fold_in(jax.random.fold_in(key, 6), axis_at), (parts,), jnp.float32, low / len(cuts), largest / len(cuts))
        gain = gain * jnp.repeat(jnp.exp(heights), shape[axis_at] // parts).reshape((-1,) + (1,) * (len(shape) - 1 - axis_at))
    return gain


def centred(rng, extent, spread, reach, cuts=(), kind=jnp.bfloat16):
    entries = jax.random.normal(rng, extent, jnp.float32) * spread
    if len(cuts) > 0:
        entries = block_scale(rng, extent, cuts, -0.22, 0.18) * entries
    return jnp.clip(entries, min=-reach, max=reach).astype(kind)


def noise_with(rng, dims, spread, limit, cuts, heavy, kind=jnp.bfloat16):
    array = spread * jax.random.normal(rng, dims, jnp.float32)
    if cuts:
        array = array * block_scale(rng, dims, cuts, -0.22, 0.18)
    return jnp.clip(strengthened(array, jax.random.fold_in(rng, 3), *heavy), -limit, limit).astype(kind)


def setup_inputs(seed: int = 0) -> dict:
    splits = jax.random.split(jax.random.key(seed), 9)
    return {
        "micro_grads": noise_with(splits[0], (N_DP, MB, D, D), 1.0, 16.0, ((0, 64), (3, 8)), (0, 2, 64, 4.0)),
        "master": centred(splits[1], (D, D), D ** -0.5, 0.21875, ((0, 64), (1, 8)), jnp.float32),
        "moment": centred(splits[2], (D, D), 0.1, 1.5, ((0, 64), (1, 8)), jnp.float32),
        "second": jnp.clip(jnp.exp(math.log(0.1) - 4.6051702 * jax.random.uniform(splits[3], (D, D), jnp.float32) ** block_scale(splits[3], (D, D), ((0, 64), (1, 8)), -0.2, 0.2)), 0.001, 0.1),
        "left_basis": centred(splits[4], (D, D), D ** -0.5, 0.21875, ((1, 64),), jnp.float32),
        "right_basis": centred(splits[5], (D, D), D ** -0.5, 0.21875, ((1, 8),), jnp.float32),
        "left_stat": draw_left_stat(jax.random.fold_in(splits[8], 71), 0),
        "right_stat": draw_right_stat(jax.random.fold_in(splits[8], 71), 0),
    }


beta_one = 0.9
beta_two = 0.95
beta_stat = 0.95
learn_rate = 0.02
adam_eps = 1e-08
norm_eps = 1e-06
quint_a = 1.875
quint_b = -1.25
quint_c = 0.375
highest = lax.Precision.HIGHEST

def refresh(stat_new, basis_old):
    power_rows = jnp.dot(stat_new.astype(jnp.bfloat16), basis_old.astype(jnp.bfloat16), preferred_element_type=jnp.float32)
    total_sum = jnp.sum(power_rows * power_rows)
    order_count = stat_new.shape[1]
    start_x = lax.optimization_barrier((power_rows * lax.rsqrt(total_sum * (4.0 / order_count) + norm_eps)).astype(jnp.bfloat16))
    gram_mat = lax.optimization_barrier(jnp.dot(start_x, start_x.T, preferred_element_type=jnp.float32).astype(jnp.bfloat16))
    square = jnp.dot(gram_mat, gram_mat, preferred_element_type=jnp.float32)
    poly_mat = (quint_b * gram_mat.astype(jnp.float32) + quint_c * square).astype(jnp.bfloat16)
    middle = quint_a * start_x.astype(jnp.float32) + jnp.dot(poly_mat, start_x, preferred_element_type=jnp.float32)
    middle = lax.optimization_barrier(middle.astype(jnp.bfloat16))
    gram_two = jnp.dot(middle, middle.T, preferred_element_type=jnp.float32).astype(jnp.bfloat16)
    return 1.5 * middle.astype(jnp.float32) - 0.5 * jnp.dot(gram_two, middle, preferred_element_type=jnp.float32)

def reference(micro_grads, master, moment, second, left_basis, right_basis, left_stat, right_stat):
    grad_mean = lax.optimization_barrier(jnp.sum(micro_grads, axis=(0, 1), dtype=jnp.float32)) / (MB * N_DP)
    new_moment = beta_one * moment + (1.0 - beta_one) * grad_mean

    def rotate(matrix):
        left_part = jnp.dot(left_basis.T, matrix, precision=highest)
        return jnp.dot(left_part, right_basis, precision=highest)
    rot_grad = rotate(grad_mean)
    rot_moment = rotate(new_moment)
    new_second = beta_two * second + (1.0 - beta_two) * rot_grad * rot_grad
    rot_step = rot_moment / (jnp.sqrt(new_second) + adam_eps)
    step_full = jnp.dot(jnp.dot(left_basis, rot_step, precision=highest), right_basis.T, precision=highest)
    new_master = master - learn_rate * step_full
    weights_block = new_master.astype(jnp.bfloat16)
    new_left_stat = beta_stat * left_stat + (1.0 - beta_stat) * jnp.dot(grad_mean, grad_mean.T, precision=highest)
    new_right_stat = beta_stat * right_stat + (1.0 - beta_stat) * jnp.dot(grad_mean.T, grad_mean, precision=highest)
    new_left_basis = refresh(new_left_stat, left_basis)
    new_right_basis = refresh(new_right_stat, right_basis)
    return (weights_block, new_master, new_moment, new_second, new_left_stat, new_right_stat, new_left_basis, new_right_basis)
```

```python
import jax
import jax.numpy as jnp
from jax import lax
from jax.sharding import PartitionSpec as P

beta_one = 0.9
beta_two = 0.95
beta_stat = 0.95
learn_rate = 0.02
adam_eps = 1e-08
norm_eps = 1e-06
quint_a = 1.875
quint_b = -1.25
quint_c = 0.375
highest = lax.Precision.HIGHEST


def for_sending(x):

    def short(part):
        return part.astype(jnp.bfloat16) if part.dtype == jnp.float32 else part

    return jax.tree.map(short, x)


def all_rows(pair):
    return jax.tree.map(
        lambda part, own: part.astype(own.dtype),
        lax.all_gather(for_sending(pair), "mp", axis=0, tiled=True),
        pair,
    )


def row_gram(row_part, whole_part):
    return lax.dot_general(
        row_part, whole_part, (((1,), (1,)), ((), ())), preferred_element_type=jnp.float32
    )


def scatter_sum(x, axis):
    count = lax.axis_size(axis)
    chunks = x.reshape((count, x.shape[0] // count) + x.shape[1:])
    return jnp.sum(lax.all_to_all(chunks, axis, 0, 0, tiled=False), axis=0)


def gather_rows(x, axis):
    count = lax.axis_size(axis)
    return lax.all_to_all(jnp.broadcast_to(x[None], (count,) + x.shape), axis, 0, 0, tiled=False)


def per_device(micro_grads, master, moment, second, left_basis, right_basis, left_stat, right_stat):
    dp_count = lax.axis_size("dp")
    micro_count = micro_grads.shape[1]
    local_sum = jnp.sum(micro_grads[0], axis=0, dtype=jnp.float32)
    grad_piece = scatter_sum(local_sum, "dp") / (micro_count * dp_count)
    new_moment = beta_one * moment + (1.0 - beta_one) * grad_piece
    pieces = gather_rows(jnp.stack([grad_piece, new_moment]), "dp")
    pieces = jnp.swapaxes(pieces, 0, 1).reshape(2, -1, pieces.shape[-1])
    left_full = lax.all_gather(left_basis, "dp", axis=1, tiled=True)
    both_full = lax.all_gather(pieces, "mp", axis=2, tiled=True)
    right_full = lax.all_gather(right_basis, "mp", axis=1, tiled=True)
    grad_full = both_full[0]
    moment_full = both_full[1]

    def rotate(matrix):
        left_part = lax.dot_general(left_basis, matrix, (((0,), (0,)), ((), ())), precision=highest)
        return jnp.dot(left_part, right_basis, precision=highest)

    rot_grad = rotate(grad_full)
    rot_moment = rotate(moment_full)
    new_second = beta_two * second + (1.0 - beta_two) * rot_grad * rot_grad
    rot_step = rot_moment / (jnp.sqrt(new_second) + adam_eps)
    back_half = scatter_sum(
        lax.dot_general(right_basis, rot_step, (((1,), (1,)), ((), ())), precision=highest),
        "mp",
    )
    step_piece = scatter_sum(
        lax.dot_general(left_basis, back_half, (((1,), (1,)), ((), ())), precision=highest),
        "dp",
    )
    new_master = master - learn_rate * step_piece
    weights_block = gather_rows(new_master.astype(jnp.bfloat16), "dp").reshape(
        -1, new_master.shape[1]
    )
    band_width = right_basis.shape[1]
    band_start = lax.axis_index("mp") * band_width
    grad_band = lax.dynamic_slice_in_dim(grad_full, band_start, band_width, 0)
    grad_strip = lax.dynamic_slice_in_dim(grad_full, band_start, band_width, 1)
    left_outer = lax.dot_general(grad_band, grad_full, (((1,), (1,)), ((), ())), precision=highest)
    right_outer = lax.dot_general(
        grad_strip, grad_full, (((0,), (0,)), ((), ())), precision=highest
    )
    new_left_stat = beta_stat * left_stat + (1.0 - beta_stat) * left_outer
    new_right_stat = beta_stat * right_stat + (1.0 - beta_stat) * right_outer
    order_count = left_stat.shape[1]
    power_left = jnp.dot(
        new_left_stat.astype(jnp.bfloat16),
        left_full.astype(jnp.bfloat16),
        preferred_element_type=jnp.float32,
    )
    power_right = jnp.dot(
        new_right_stat.astype(jnp.bfloat16),
        right_full.astype(jnp.bfloat16),
        preferred_element_type=jnp.float32,
    )
    total_left, total_right = lax.psum(
        (jnp.sum(power_left * power_left), jnp.sum(power_right * power_right)), "mp"
    )
    start_left = lax.optimization_barrier(
        (power_left * lax.rsqrt(total_left * (4.0 / order_count) + norm_eps)).astype(jnp.bfloat16)
    )
    start_right = lax.optimization_barrier(
        (power_right * lax.rsqrt(total_right * (4.0 / order_count) + norm_eps)).astype(jnp.bfloat16)
    )
    start_rows = (start_left, start_right)
    start_whole = all_rows(start_rows)
    gram_rows = tuple(
        (
            lax.optimization_barrier(row_gram(row_part, whole_part).astype(jnp.bfloat16))
            for row_part, whole_part in zip(start_rows, start_whole)
        )
    )
    gram_whole = all_rows(gram_rows)
    middle_rows = []
    for row_part, gram_part, gram_all, whole_part in zip(
        start_rows, gram_rows, gram_whole, start_whole
    ):
        square = jnp.dot(gram_part, gram_all, preferred_element_type=jnp.float32)
        poly_rows = (quint_b * gram_part.astype(jnp.float32) + quint_c * square).astype(
            jnp.bfloat16
        )
        middle = quint_a * row_part.astype(jnp.float32) + jnp.dot(
            poly_rows, whole_part, preferred_element_type=jnp.float32
        )
        middle_rows.append(lax.optimization_barrier(middle.astype(jnp.bfloat16)))
    middle_whole = all_rows(tuple(middle_rows))
    new_bases = []
    for row_part, whole_part in zip(middle_rows, middle_whole):
        gram_two = row_gram(row_part, whole_part).astype(jnp.bfloat16)
        new_bases.append(
            1.5 * row_part.astype(jnp.float32)
            - 0.5 * jnp.dot(gram_two, whole_part, preferred_element_type=jnp.float32)
        )
    return (
        weights_block,
        new_master,
        new_moment,
        new_second,
        new_left_stat,
        new_right_stat,
        new_bases[0],
        new_bases[1],
    )


def solution(mesh):
    in_specs = (
        P("dp", None, None, "mp"),
        P("dp", "mp"),
        P("dp", "mp"),
        P("dp", "mp"),
        P(None, "dp"),
        P(None, "mp"),
        P("mp", None),
        P("mp", None),
    )
    out_specs = (
        P(None, "mp"),
        P("dp", "mp"),
        P("dp", "mp"),
        P("dp", "mp"),
        P("mp", None),
        P("mp", None),
        P("mp", None),
        P("mp", None),
    )
    return jax.shard_map(
        per_device, mesh=mesh, in_specs=in_specs, out_specs=out_specs, check_vma=False
    )
```

```python
import jax
import jax.numpy as jnp
from jax import lax
from jax.sharding import PartitionSpec as P

beta_one = 0.9
beta_two = 0.95
beta_stat = 0.95
learn_rate = 0.02
adam_eps = 1e-08
norm_eps = 1e-06
quint_a = 1.875
quint_b = -1.25
quint_c = 0.375
highest = lax.Precision.HIGHEST


def for_sending(x):

    def short(part):
        return part.astype(jnp.bfloat16) if part.dtype == jnp.float32 else part

    return jax.tree.map(short, x)


def all_rows(pair):
    whole = lax.all_gather(jnp.stack(for_sending(pair)), "mp", axis=1, tiled=True)
    return tuple(whole[side].astype(pair[side].dtype) for side in range(len(pair)))


def row_gram(row_part, whole_part):
    return lax.dot_general(
        row_part, whole_part, (((1,), (1,)), ((), ())), preferred_element_type=jnp.float32
    )


def scatter_sum(x, axis):
    count = lax.axis_size(axis)
    chunks = x.reshape((count, x.shape[0] // count) + x.shape[1:])
    return jnp.sum(lax.all_to_all(chunks, axis, 0, 0, tiled=False), axis=0)


def gather_rows(x, axis):
    count = lax.axis_size(axis)
    return lax.all_to_all(jnp.broadcast_to(x[None], (count,) + x.shape), axis, 0, 0, tiled=False)


def per_device(micro_grads, master, moment, second, left_basis, right_basis, left_stat, right_stat):
    dp_count = lax.axis_size("dp")
    micro_count = micro_grads.shape[1]
    local_sum = jnp.sum(micro_grads[0], axis=0, dtype=jnp.float32)
    grad_piece = scatter_sum(local_sum, "dp") / (micro_count * dp_count)
    new_moment = beta_one * moment + (1.0 - beta_one) * grad_piece
    pieces = gather_rows(jnp.stack([grad_piece, new_moment]), "dp")
    pieces = jnp.swapaxes(pieces, 0, 1).reshape(2, -1, pieces.shape[-1])
    left_cols = gather_rows(left_basis.astype(jnp.bfloat16), "dp")
    left_full = jnp.moveaxis(left_cols, 0, 1).reshape(left_basis.shape[0], -1)
    both_full = lax.all_gather(pieces, "mp", axis=2, tiled=True)
    right_full = lax.all_gather(right_basis, "mp", axis=1, tiled=True)
    grad_full = both_full[0]
    moment_full = both_full[1]

    def rotate(matrix):
        left_part = lax.dot_general(left_basis, matrix, (((0,), (0,)), ((), ())), precision=highest)
        return jnp.dot(left_part, right_basis, precision=highest)

    rot_grad = rotate(grad_full)
    rot_moment = rotate(moment_full)
    new_second = beta_two * second + (1.0 - beta_two) * rot_grad * rot_grad
    rot_step = rot_moment / (jnp.sqrt(new_second) + adam_eps)
    back_half = scatter_sum(
        lax.dot_general(right_basis, rot_step, (((1,), (1,)), ((), ())), precision=highest),
        "mp",
    )
    step_piece = scatter_sum(
        lax.dot_general(left_basis, back_half, (((1,), (1,)), ((), ())), precision=highest),
        "dp",
    )
    new_master = master - learn_rate * step_piece
    weights_block = gather_rows(new_master.astype(jnp.bfloat16), "dp").reshape(
        -1, new_master.shape[1]
    )
    band_width = right_basis.shape[1]
    band_start = lax.axis_index("mp") * band_width
    grad_band = lax.dynamic_slice_in_dim(grad_full, band_start, band_width, 0)
    grad_strip = lax.dynamic_slice_in_dim(grad_full, band_start, band_width, 1)
    left_outer = lax.dot_general(grad_band, grad_full, (((1,), (1,)), ((), ())), precision=highest)
    right_outer = lax.dot_general(
        grad_strip, grad_full, (((0,), (0,)), ((), ())), precision=highest
    )
    new_left_stat = beta_stat * left_stat + (1.0 - beta_stat) * left_outer
    new_right_stat = beta_stat * right_stat + (1.0 - beta_stat) * right_outer
    order_count = left_stat.shape[1]
    power_left = jnp.dot(
        new_left_stat.astype(jnp.bfloat16),
        left_full.astype(jnp.bfloat16),
        preferred_element_type=jnp.float32,
    )
    power_right = jnp.dot(
        new_right_stat.astype(jnp.bfloat16),
        right_full.astype(jnp.bfloat16),
        preferred_element_type=jnp.float32,
    )
    total_left, total_right = lax.psum(
        (jnp.sum(power_left * power_left), jnp.sum(power_right * power_right)), "mp"
    )
    start_left = lax.optimization_barrier(
        (power_left * lax.rsqrt(total_left * (4.0 / order_count) + norm_eps)).astype(jnp.bfloat16)
    )
    start_right = lax.optimization_barrier(
        (power_right * lax.rsqrt(total_right * (4.0 / order_count) + norm_eps)).astype(jnp.bfloat16)
    )
    start_rows = (start_left, start_right)
    start_whole = all_rows(start_rows)
    gram_rows = tuple(
        (
            lax.optimization_barrier(row_gram(row_part, whole_part).astype(jnp.bfloat16))
            for row_part, whole_part in zip(start_rows, start_whole)
        )
    )
    gram_whole = all_rows(gram_rows)
    middle_rows = []
    for row_part, gram_part, gram_all, whole_part in zip(
        start_rows, gram_rows, gram_whole, start_whole
    ):
        square = jnp.dot(gram_part, gram_all, preferred_element_type=jnp.float32)
        poly_rows = (quint_b * gram_part.astype(jnp.float32) + quint_c * square).astype(
            jnp.bfloat16
        )
        middle = quint_a * row_part.astype(jnp.float32) + jnp.dot(
            poly_rows, whole_part, preferred_element_type=jnp.float32
        )
        middle_rows.append(lax.optimization_barrier(middle.astype(jnp.bfloat16)))
    middle_whole = all_rows(tuple(middle_rows))
    new_bases = []
    for row_part, whole_part in zip(middle_rows, middle_whole):
        gram_two = row_gram(row_part, whole_part).astype(jnp.bfloat16)
        new_bases.append(
            1.5 * row_part.astype(jnp.float32)
            - 0.5 * jnp.dot(gram_two, whole_part, preferred_element_type=jnp.float32)
        )
    return (
        weights_block,
        new_master,
        new_moment,
        new_second,
        new_left_stat,
        new_right_stat,
        new_bases[0],
        new_bases[1],
    )


def solution(mesh):
    in_specs = (
        P("dp", None, None, "mp"),
        P("dp", "mp"),
        P("dp", "mp"),
        P("dp", "mp"),
        P(None, "dp"),
        P(None, "mp"),
        P("mp", None),
        P("mp", None),
    )
    out_specs = (
        P(None, "mp"),
        P("dp", "mp"),
        P("dp", "mp"),
        P("dp", "mp"),
        P("mp", None),
        P("mp", None),
        P("mp", None),
        P("mp", None),
    )
    return jax.shard_map(
        per_device, mesh=mesh, in_specs=in_specs, out_specs=out_specs, check_vma=False
    )
```

```python
import jax
import jax.numpy as jnp
from jax import lax
from jax.sharding import PartitionSpec as P

beta_one = 0.9
beta_two = 0.95
beta_stat = 0.95
learn_rate = 0.02
adam_eps = 1e-08
norm_eps = 1e-06
quint_a = 1.875
quint_b = -1.25
quint_c = 0.375
highest = lax.Precision.HIGHEST


def for_sending(x):

    def short(part):
        return part.astype(jnp.bfloat16) if part.dtype == jnp.float32 else part

    return jax.tree.map(short, x)


def all_rows(pair):
    whole = lax.all_gather(jnp.stack(for_sending(pair)), "mp", axis=1, tiled=True)
    return tuple(whole[side].astype(pair[side].dtype) for side in range(len(pair)))


def row_gram(row_part, whole_part):
    return lax.dot_general(
        row_part, whole_part, (((1,), (1,)), ((), ())), preferred_element_type=jnp.float32
    )


def scatter_sum(x, axis):
    count = lax.axis_size(axis)
    chunks = x.reshape((count, x.shape[0] // count) + x.shape[1:])
    return jnp.sum(lax.all_to_all(chunks, axis, 0, 0, tiled=False), axis=0)


def gather_rows(x, axis):
    count = lax.axis_size(axis)
    return lax.all_to_all(jnp.broadcast_to(x[None], (count,) + x.shape), axis, 0, 0, tiled=False)


def per_device(micro_grads, master, moment, second, left_basis, right_basis, left_stat, right_stat):
    dp_count = lax.axis_size("dp")
    micro_count = micro_grads.shape[1]
    local_sum = jnp.sum(micro_grads[0], axis=0, dtype=jnp.float32)
    grad_piece = scatter_sum(local_sum, "dp") / (micro_count * dp_count)
    new_moment = beta_one * moment + (1.0 - beta_one) * grad_piece
    pieces = gather_rows(jnp.stack([grad_piece, new_moment]), "dp")
    pieces = jnp.swapaxes(pieces, 0, 1).reshape(2, -1, pieces.shape[-1])
    left_cols = gather_rows(left_basis.astype(jnp.bfloat16), "dp")
    left_full = jnp.moveaxis(left_cols, 0, 1).reshape(left_basis.shape[0], -1)
    right_full = lax.all_gather(right_basis, "mp", axis=1, tiled=True)
    pieces, right_full = lax.optimization_barrier((pieces, right_full))
    both_full = lax.all_gather(pieces, "mp", axis=2, tiled=True)
    grad_full = both_full[0]
    moment_full = both_full[1]

    def rotate(matrix):
        left_part = lax.dot_general(left_basis, matrix, (((0,), (0,)), ((), ())), precision=highest)
        return jnp.dot(left_part, right_basis, precision=highest)

    rot_grad = rotate(grad_full)
    rot_moment = rotate(moment_full)
    new_second = beta_two * second + (1.0 - beta_two) * rot_grad * rot_grad
    rot_step = rot_moment / (jnp.sqrt(new_second) + adam_eps)
    band_width = right_basis.shape[1]
    band_start = lax.axis_index("mp") * band_width
    grad_band = lax.dynamic_slice_in_dim(grad_full, band_start, band_width, 0)
    grad_strip = lax.dynamic_slice_in_dim(grad_full, band_start, band_width, 1)
    left_outer = lax.dot_general(grad_band, grad_full, (((1,), (1,)), ((), ())), precision=highest)
    right_outer = lax.dot_general(
        grad_strip, grad_full, (((0,), (0,)), ((), ())), precision=highest
    )
    new_left_stat = beta_stat * left_stat + (1.0 - beta_stat) * left_outer
    new_right_stat = beta_stat * right_stat + (1.0 - beta_stat) * right_outer
    order_count = left_stat.shape[1]
    power_left = jnp.dot(
        new_left_stat.astype(jnp.bfloat16),
        left_full.astype(jnp.bfloat16),
        preferred_element_type=jnp.float32,
    )
    power_right = jnp.dot(
        new_right_stat.astype(jnp.bfloat16),
        right_full.astype(jnp.bfloat16),
        preferred_element_type=jnp.float32,
    )
    total_left, total_right = lax.psum(
        (jnp.sum(power_left * power_left), jnp.sum(power_right * power_right)), "mp"
    )
    start_left = lax.optimization_barrier(
        (power_left * lax.rsqrt(total_left * (4.0 / order_count) + norm_eps)).astype(jnp.bfloat16)
    )
    start_right = lax.optimization_barrier(
        (power_right * lax.rsqrt(total_right * (4.0 / order_count) + norm_eps)).astype(jnp.bfloat16)
    )
    start_rows = (start_left, start_right)
    rot_step, start_rows = lax.optimization_barrier((rot_step, start_rows))
    start_whole = all_rows(start_rows)
    back_half = scatter_sum(
        lax.dot_general(right_basis, rot_step, (((1,), (1,)), ((), ())), precision=highest),
        "mp",
    )
    step_piece = scatter_sum(
        lax.dot_general(left_basis, back_half, (((1,), (1,)), ((), ())), precision=highest),
        "dp",
    )
    new_master = master - learn_rate * step_piece
    weights_block = gather_rows(new_master.astype(jnp.bfloat16), "dp").reshape(
        -1, new_master.shape[1]
    )
    start_whole, weights_block, new_master = lax.optimization_barrier(
        (start_whole, weights_block, new_master)
    )
    new_bases = []
    for whole_part in start_whole:
        gram = lax.optimization_barrier(row_gram(whole_part, whole_part).astype(jnp.bfloat16))
        square = jnp.dot(gram, gram, preferred_element_type=jnp.float32)
        poly = (quint_b * gram.astype(jnp.float32) + quint_c * square).astype(jnp.bfloat16)
        middle = quint_a * whole_part.astype(jnp.float32) + jnp.dot(
            poly, whole_part, preferred_element_type=jnp.float32
        )
        middle = lax.optimization_barrier(middle.astype(jnp.bfloat16))
        middle_rows = lax.dynamic_slice_in_dim(middle, band_start, band_width, 0)
        gram_two = row_gram(middle_rows, middle).astype(jnp.bfloat16)
        new_bases.append(
            1.5 * middle_rows.astype(jnp.float32)
            - 0.5 * jnp.dot(gram_two, middle, preferred_element_type=jnp.float32)
        )
    return (
        weights_block,
        new_master,
        new_moment,
        new_second,
        new_left_stat,
        new_right_stat,
        new_bases[0],
        new_bases[1],
    )


def solution(mesh):
    in_specs = (
        P("dp", None, None, "mp"),
        P("dp", "mp"),
        P("dp", "mp"),
        P("dp", "mp"),
        P(None, "dp"),
        P(None, "mp"),
        P("mp", None),
        P("mp", None),
    )
    out_specs = (
        P(None, "mp"),
        P("dp", "mp"),
        P("dp", "mp"),
        P("dp", "mp"),
        P("mp", None),
        P("mp", None),
        P("mp", None),
        P("mp", None),
    )
    return jax.shard_map(
        per_device, mesh=mesh, in_specs=in_specs, out_specs=out_specs, check_vma=False
    )
```

```python
import jax
import jax.numpy as jnp
from jax import lax
from jax.sharding import PartitionSpec as P

beta_one = 0.9
beta_two = 0.95
beta_stat = 0.95
learn_rate = 0.02
adam_eps = 1e-08
norm_eps = 1e-06
quint_a = 1.875
quint_b = -1.25
quint_c = 0.375
highest = lax.Precision.HIGHEST


def row_gram(row_part, whole_part):
    return lax.dot_general(
        row_part, whole_part, (((1,), (1,)), ((), ())), preferred_element_type=jnp.float32
    )


def scatter_sum(x, axis):
    count = lax.axis_size(axis)
    chunks = x.reshape((count, x.shape[0] // count) + x.shape[1:])
    return jnp.sum(lax.all_to_all(chunks, axis, 0, 0, tiled=False), axis=0)


def gather_rows(x, axis):
    count = lax.axis_size(axis)
    return lax.all_to_all(jnp.broadcast_to(x[None], (count,) + x.shape), axis, 0, 0, tiled=False)


def per_device(micro_grads, master, moment, second, left_basis, right_basis, left_stat, right_stat):
    dp_count = lax.axis_size("dp")
    micro_count = micro_grads.shape[1]
    local_sum = jnp.sum(micro_grads[0], axis=0, dtype=jnp.float32)
    grad_piece = scatter_sum(local_sum, "dp") / (micro_count * dp_count)
    new_moment = beta_one * moment + (1.0 - beta_one) * grad_piece
    pieces = gather_rows(jnp.stack([grad_piece, new_moment]), "dp")
    pieces = jnp.swapaxes(pieces, 0, 1).reshape(2, -1, pieces.shape[-1])
    left_cols = gather_rows(left_basis.astype(jnp.bfloat16), "dp")
    left_full = jnp.moveaxis(left_cols, 0, 1).reshape(left_basis.shape[0], -1)
    right_full = lax.all_gather(right_basis, "mp", axis=1, tiled=True)
    pieces, right_full = lax.optimization_barrier((pieces, right_full))
    both_full = lax.all_gather(pieces, "mp", axis=2, tiled=True)
    grad_full = both_full[0]
    moment_full = both_full[1]

    def rotate(matrix):
        left_part = lax.dot_general(left_basis, matrix, (((0,), (0,)), ((), ())), precision=highest)
        return jnp.dot(left_part, right_basis, precision=highest)

    rot_grad = rotate(grad_full)
    rot_moment = rotate(moment_full)
    new_second = beta_two * second + (1.0 - beta_two) * rot_grad * rot_grad
    rot_step = rot_moment / (jnp.sqrt(new_second) + adam_eps)
    band_width = right_basis.shape[1]
    band_start = lax.axis_index("mp") * band_width
    grad_band = lax.dynamic_slice_in_dim(grad_full, band_start, band_width, 0)
    grad_strip = lax.dynamic_slice_in_dim(grad_full, band_start, band_width, 1)
    left_outer = lax.dot_general(grad_band, grad_full, (((1,), (1,)), ((), ())), precision=highest)
    right_outer = lax.dot_general(
        grad_strip, grad_full, (((0,), (0,)), ((), ())), precision=highest
    )
    new_left_stat = beta_stat * left_stat + (1.0 - beta_stat) * left_outer
    new_right_stat = beta_stat * right_stat + (1.0 - beta_stat) * right_outer
    order_count = left_stat.shape[1]
    power_left = jnp.dot(
        new_left_stat.astype(jnp.bfloat16),
        left_full.astype(jnp.bfloat16),
        preferred_element_type=jnp.float32,
    )
    power_right = jnp.dot(
        new_right_stat.astype(jnp.bfloat16),
        right_full.astype(jnp.bfloat16),
        preferred_element_type=jnp.float32,
    )
    power_rows = jnp.stack([power_left, power_right])
    rot_step, power_rows = lax.optimization_barrier((rot_step, power_rows))
    power_whole = lax.all_gather(power_rows, "mp", axis=1, tiled=True)
    back_half = scatter_sum(
        lax.dot_general(right_basis, rot_step, (((1,), (1,)), ((), ())), precision=highest),
        "mp",
    )
    step_piece = scatter_sum(
        lax.dot_general(left_basis, back_half, (((1,), (1,)), ((), ())), precision=highest),
        "dp",
    )
    new_master = master - learn_rate * step_piece
    weights_block = gather_rows(new_master.astype(jnp.bfloat16), "dp").reshape(
        -1, new_master.shape[1]
    )
    new_bases = []
    for power_part in power_whole:
        total = jnp.sum(power_part * power_part)
        whole_part = lax.optimization_barrier(
            (power_part * lax.rsqrt(total * (4.0 / order_count) + norm_eps)).astype(jnp.bfloat16)
        )
        gram = lax.optimization_barrier(row_gram(whole_part, whole_part).astype(jnp.bfloat16))
        square = jnp.dot(gram, gram, preferred_element_type=jnp.float32)
        poly = (quint_b * gram.astype(jnp.float32) + quint_c * square).astype(jnp.bfloat16)
        middle = quint_a * whole_part.astype(jnp.float32) + jnp.dot(
            poly, whole_part, preferred_element_type=jnp.float32
        )
        middle = lax.optimization_barrier(middle.astype(jnp.bfloat16))
        middle_rows = lax.dynamic_slice_in_dim(middle, band_start, band_width, 0)
        gram_two = row_gram(middle_rows, middle).astype(jnp.bfloat16)
        new_bases.append(
            1.5 * middle_rows.astype(jnp.float32)
            - 0.5 * jnp.dot(gram_two, middle, preferred_element_type=jnp.float32)
        )
    return (
        weights_block,
        new_master,
        new_moment,
        new_second,
        new_left_stat,
        new_right_stat,
        new_bases[0],
        new_bases[1],
    )


def solution(mesh):
    in_specs = (
        P("dp", None, None, "mp"),
        P("dp", "mp"),
        P("dp", "mp"),
        P("dp", "mp"),
        P(None, "dp"),
        P(None, "mp"),
        P("mp", None),
        P("mp", None),
    )
    out_specs = (
        P(None, "mp"),
        P("dp", "mp"),
        P("dp", "mp"),
        P("dp", "mp"),
        P("mp", None),
        P("mp", None),
        P("mp", None),
        P("mp", None),
    )
    return jax.shard_map(
        per_device, mesh=mesh, in_specs=in_specs, out_specs=out_specs, check_vma=False
    )
```

```python
import jax
import jax.numpy as jnp
from jax import lax
from jax.sharding import PartitionSpec as P

beta_one = 0.9
beta_two = 0.95
beta_stat = 0.95
learn_rate = 0.02
adam_eps = 1e-08
norm_eps = 1e-06
quint_a = 1.875
quint_b = -1.25
quint_c = 0.375
highest = lax.Precision.HIGHEST


def row_gram(row_part, whole_part):
    return lax.dot_general(
        row_part, whole_part, (((1,), (1,)), ((), ())), preferred_element_type=jnp.float32
    )


def scatter_sum(x, axis):
    count = lax.axis_size(axis)
    chunks = x.reshape((count, x.shape[0] // count) + x.shape[1:])
    return jnp.sum(lax.all_to_all(chunks, axis, 0, 0, tiled=False), axis=0)


def gather_rows(x, axis):
    count = lax.axis_size(axis)
    return lax.all_to_all(jnp.broadcast_to(x[None], (count,) + x.shape), axis, 0, 0, tiled=False)


def per_device(micro_grads, master, moment, second, left_basis, right_basis, left_stat, right_stat):
    dp_count = lax.axis_size("dp")
    micro_count = micro_grads.shape[1]
    local_sum = jnp.sum(micro_grads[0], axis=0, dtype=jnp.float32)
    grad_piece = scatter_sum(local_sum, "dp") / (micro_count * dp_count)
    new_moment = beta_one * moment + (1.0 - beta_one) * grad_piece
    moment_rows = gather_rows(moment, "mp")
    moment_rows = jnp.moveaxis(moment_rows, 0, 1).reshape(moment.shape[0], -1)
    moment_right = jnp.dot(moment_rows, right_basis, precision=highest)
    moment_right = gather_rows(moment_right, "dp").reshape(-1, moment.shape[1])
    moment_turned = lax.dot_general(
        left_basis, moment_right, (((0,), (0,)), ((), ())), precision=highest
    )
    pieces = gather_rows(grad_piece, "dp").reshape(-1, grad_piece.shape[1])
    left_cols = gather_rows(left_basis.astype(jnp.bfloat16), "dp")
    left_full = jnp.moveaxis(left_cols, 0, 1).reshape(left_basis.shape[0], -1)
    right_full = lax.all_gather(right_basis, "mp", axis=1, tiled=True)
    pieces, right_full = lax.optimization_barrier((pieces, right_full))
    grad_full = lax.all_gather(pieces, "mp", axis=1, tiled=True)

    def rotate(matrix):
        left_part = lax.dot_general(left_basis, matrix, (((0,), (0,)), ((), ())), precision=highest)
        return jnp.dot(left_part, right_basis, precision=highest)

    rot_grad = rotate(grad_full)
    rot_moment = beta_one * moment_turned + (1.0 - beta_one) * rot_grad
    new_second = beta_two * second + (1.0 - beta_two) * rot_grad * rot_grad
    rot_step = rot_moment / (jnp.sqrt(new_second) + adam_eps)
    band_width = right_basis.shape[1]
    band_start = lax.axis_index("mp") * band_width
    grad_band = lax.dynamic_slice_in_dim(grad_full, band_start, band_width, 0)
    grad_strip = lax.dynamic_slice_in_dim(grad_full, band_start, band_width, 1)
    left_outer = lax.dot_general(grad_band, grad_full, (((1,), (1,)), ((), ())), precision=highest)
    right_outer = lax.dot_general(
        grad_strip, grad_full, (((0,), (0,)), ((), ())), precision=highest
    )
    new_left_stat = beta_stat * left_stat + (1.0 - beta_stat) * left_outer
    new_right_stat = beta_stat * right_stat + (1.0 - beta_stat) * right_outer
    order_count = left_stat.shape[1]
    power_left = jnp.dot(
        new_left_stat.astype(jnp.bfloat16),
        left_full.astype(jnp.bfloat16),
        preferred_element_type=jnp.float32,
    )
    power_right = jnp.dot(
        new_right_stat.astype(jnp.bfloat16),
        right_full.astype(jnp.bfloat16),
        preferred_element_type=jnp.float32,
    )
    power_rows = jnp.stack([power_left, power_right])
    rot_step, power_rows = lax.optimization_barrier((rot_step, power_rows))
    power_whole = lax.all_gather(power_rows, "mp", axis=1, tiled=True)
    back_half = scatter_sum(
        lax.dot_general(right_basis, rot_step, (((1,), (1,)), ((), ())), precision=highest),
        "mp",
    )
    step_piece = scatter_sum(
        lax.dot_general(left_basis, back_half, (((1,), (1,)), ((), ())), precision=highest),
        "dp",
    )
    new_master = master - learn_rate * step_piece
    weights_block = gather_rows(new_master.astype(jnp.bfloat16), "dp").reshape(
        -1, new_master.shape[1]
    )
    new_bases = []
    for power_part in power_whole:
        total = jnp.sum(power_part * power_part)
        whole_part = lax.optimization_barrier(
            (power_part * lax.rsqrt(total * (4.0 / order_count) + norm_eps)).astype(jnp.bfloat16)
        )
        gram = lax.optimization_barrier(row_gram(whole_part, whole_part).astype(jnp.bfloat16))
        square = jnp.dot(gram, gram, preferred_element_type=jnp.float32)
        poly = (quint_b * gram.astype(jnp.float32) + quint_c * square).astype(jnp.bfloat16)
        middle = quint_a * whole_part.astype(jnp.float32) + jnp.dot(
            poly, whole_part, preferred_element_type=jnp.float32
        )
        middle = lax.optimization_barrier(middle.astype(jnp.bfloat16))
        middle_rows = lax.dynamic_slice_in_dim(middle, band_start, band_width, 0)
        gram_two = row_gram(middle_rows, middle).astype(jnp.bfloat16)
        new_bases.append(
            1.5 * middle_rows.astype(jnp.float32)
            - 0.5 * jnp.dot(gram_two, middle, preferred_element_type=jnp.float32)
        )
    return (
        weights_block,
        new_master,
        new_moment,
        new_second,
        new_left_stat,
        new_right_stat,
        new_bases[0],
        new_bases[1],
    )


def solution(mesh):
    in_specs = (
        P("dp", None, None, "mp"),
        P("dp", "mp"),
        P("dp", "mp"),
        P("dp", "mp"),
        P(None, "dp"),
        P(None, "mp"),
        P("mp", None),
        P("mp", None),
    )
    out_specs = (
        P(None, "mp"),
        P("dp", "mp"),
        P("dp", "mp"),
        P("dp", "mp"),
        P("mp", None),
        P("mp", None),
        P("mp", None),
        P("mp", None),
    )
    return jax.shard_map(
        per_device, mesh=mesh, in_specs=in_specs, out_specs=out_specs, check_vma=False
    )
```

```python
import jax
import jax.numpy as jnp
from jax import lax
from jax.sharding import PartitionSpec as P

beta_one = 0.9
beta_two = 0.95
beta_stat = 0.95
learn_rate = 0.02
adam_eps = 1e-08
norm_eps = 1e-06
quint_a = 1.875
quint_b = -1.25
quint_c = 0.375
highest = lax.Precision.HIGHEST


def row_gram(row_part, whole_part):
    return lax.dot_general(
        row_part, whole_part, (((1,), (1,)), ((), ())), preferred_element_type=jnp.float32
    )


def scatter_sum(x, axis):
    count = lax.axis_size(axis)
    chunks = x.reshape((count, x.shape[0] // count) + x.shape[1:])
    return jnp.sum(lax.all_to_all(chunks, axis, 0, 0, tiled=False), axis=0)


def gather_rows(x, axis):
    count = lax.axis_size(axis)
    return lax.all_to_all(jnp.broadcast_to(x[None], (count,) + x.shape), axis, 0, 0, tiled=False)


def per_device(micro_grads, master, moment, second, left_basis, right_basis, left_stat, right_stat):
    dp_count = lax.axis_size("dp")
    micro_count = micro_grads.shape[1]
    local_sum = jnp.sum(micro_grads[0], axis=0, dtype=jnp.float32)
    grad_piece = scatter_sum(local_sum, "dp") / (micro_count * dp_count)
    new_moment = beta_one * moment + (1.0 - beta_one) * grad_piece
    pieces = gather_rows(jnp.stack([grad_piece, new_moment]), "dp")
    pieces = jnp.swapaxes(pieces, 0, 1).reshape(2, -1, pieces.shape[-1])
    left_cols = gather_rows(left_basis.astype(jnp.bfloat16), "dp")
    left_full = jnp.moveaxis(left_cols, 0, 1).reshape(left_basis.shape[0], -1)
    right_full = lax.all_gather(right_basis, "mp", axis=1, tiled=True)
    pieces, right_full = lax.optimization_barrier((pieces, right_full))
    both_full = lax.all_gather(pieces, "mp", axis=2, tiled=True)
    grad_full = both_full[0]
    moment_full = both_full[1]

    def rotate(matrix):
        left_part = lax.dot_general(left_basis, matrix, (((0,), (0,)), ((), ())), precision=highest)
        return jnp.dot(left_part, right_basis, precision=highest)

    rot_grad = rotate(grad_full)
    rot_moment = rotate(moment_full)
    new_second = beta_two * second + (1.0 - beta_two) * rot_grad * rot_grad
    rot_step = rot_moment / (jnp.sqrt(new_second) + adam_eps)
    band_width = right_basis.shape[1]
    band_start = lax.axis_index("mp") * band_width
    grad_band = lax.dynamic_slice_in_dim(grad_full, band_start, band_width, 0)
    grad_strip = lax.dynamic_slice_in_dim(grad_full, band_start, band_width, 1)
    left_outer = lax.dot_general(grad_band, grad_full, (((1,), (1,)), ((), ())), precision=highest)
    right_outer = lax.dot_general(
        grad_strip, grad_full, (((0,), (0,)), ((), ())), precision=highest
    )
    new_left_stat = beta_stat * left_stat + (1.0 - beta_stat) * left_outer
    new_right_stat = beta_stat * right_stat + (1.0 - beta_stat) * right_outer
    order_count = left_stat.shape[1]
    stat_rows = jnp.stack([new_left_stat, new_right_stat]).astype(jnp.bfloat16)
    rot_step, stat_rows = lax.optimization_barrier((rot_step, stat_rows))
    stat_whole = lax.all_gather(stat_rows, "mp", axis=1, tiled=True)
    back_half = scatter_sum(
        lax.dot_general(right_basis, rot_step, (((1,), (1,)), ((), ())), precision=highest),
        "mp",
    )
    step_piece = scatter_sum(
        lax.dot_general(left_basis, back_half, (((1,), (1,)), ((), ())), precision=highest),
        "dp",
    )
    new_master = master - learn_rate * step_piece
    weights_block = gather_rows(new_master.astype(jnp.bfloat16), "dp").reshape(
        -1, new_master.shape[1]
    )
    new_bases = []
    for stat_part, basis_part in zip(stat_whole, (left_full, right_full)):
        power_part = jnp.dot(
            stat_part, basis_part.astype(jnp.bfloat16), preferred_element_type=jnp.float32
        )
        total = jnp.sum(power_part * power_part)
        whole_part = lax.optimization_barrier(
            (power_part * lax.rsqrt(total * (4.0 / order_count) + norm_eps)).astype(jnp.bfloat16)
        )
        gram = lax.optimization_barrier(row_gram(whole_part, whole_part).astype(jnp.bfloat16))
        square = jnp.dot(gram, gram, preferred_element_type=jnp.float32)
        poly = (quint_b * gram.astype(jnp.float32) + quint_c * square).astype(jnp.bfloat16)
        middle = quint_a * whole_part.astype(jnp.float32) + jnp.dot(
            poly, whole_part, preferred_element_type=jnp.float32
        )
        middle = lax.optimization_barrier(middle.astype(jnp.bfloat16))
        middle_rows = lax.dynamic_slice_in_dim(middle, band_start, band_width, 0)
        gram_two = row_gram(middle_rows, middle).astype(jnp.bfloat16)
        new_bases.append(
            1.5 * middle_rows.astype(jnp.float32)
            - 0.5 * jnp.dot(gram_two, middle, preferred_element_type=jnp.float32)
        )
    return (
        weights_block,
        new_master,
        new_moment,
        new_second,
        new_left_stat,
        new_right_stat,
        new_bases[0],
        new_bases[1],
    )


def solution(mesh):
    in_specs = (
        P("dp", None, None, "mp"),
        P("dp", "mp"),
        P("dp", "mp"),
        P("dp", "mp"),
        P(None, "dp"),
        P(None, "mp"),
        P("mp", None),
        P("mp", None),
    )
    out_specs = (
        P(None, "mp"),
        P("dp", "mp"),
        P("dp", "mp"),
        P("dp", "mp"),
        P("mp", None),
        P("mp", None),
        P("mp", None),
        P("mp", None),
    )
    return jax.shard_map(
        per_device, mesh=mesh, in_specs=in_specs, out_specs=out_specs, check_vma=False
    )
```

```python
import jax
import jax.numpy as jnp
from jax import lax
from jax.sharding import PartitionSpec as P

beta_one = 0.9
beta_two = 0.95
beta_stat = 0.95
learn_rate = 0.02
adam_eps = 1e-08
norm_eps = 1e-06
quint_a = 1.875
quint_b = -1.25
quint_c = 0.375
highest = lax.Precision.HIGHEST


def row_gram(row_part, whole_part):
    return lax.dot_general(
        row_part, whole_part, (((1,), (1,)), ((), ())), preferred_element_type=jnp.float32
    )


def scatter_sum(x, axis):
    count = lax.axis_size(axis)
    chunks = x.reshape((count, x.shape[0] // count) + x.shape[1:])
    return jnp.sum(lax.all_to_all(chunks, axis, 0, 0, tiled=False), axis=0)


def gather_rows(x, axis):
    count = lax.axis_size(axis)
    return lax.all_to_all(jnp.broadcast_to(x[None], (count,) + x.shape), axis, 0, 0, tiled=False)


def per_device(micro_grads, master, moment, second, left_basis, right_basis, left_stat, right_stat):
    dp_count = lax.axis_size("dp")
    micro_count = micro_grads.shape[1]
    local_sum = jnp.sum(micro_grads[0], axis=0, dtype=jnp.float32)
    grad_piece = scatter_sum(local_sum, "dp") / (micro_count * dp_count)
    new_moment = beta_one * moment + (1.0 - beta_one) * grad_piece
    pieces = gather_rows(jnp.stack([grad_piece, new_moment]), "dp")
    pieces = jnp.swapaxes(pieces, 0, 1).reshape(2, -1, pieces.shape[-1])
    left_cols = gather_rows(left_basis.astype(jnp.bfloat16), "dp")
    left_full = jnp.moveaxis(left_cols, 0, 1).reshape(left_basis.shape[0], -1)
    right_full = lax.all_gather(right_basis, "mp", axis=1, tiled=True)
    pieces, right_full = lax.optimization_barrier((pieces, right_full))
    both_full = lax.all_gather(pieces, "mp", axis=2, tiled=True)
    both_full, left_full = lax.optimization_barrier((both_full, left_full))
    grad_full = both_full[0]
    moment_full = both_full[1]

    def rotate(matrix):
        left_part = lax.dot_general(left_basis, matrix, (((0,), (0,)), ((), ())), precision=highest)
        return jnp.dot(left_part, right_basis, precision=highest)

    rot_grad = rotate(grad_full)
    rot_moment = rotate(moment_full)
    new_second = beta_two * second + (1.0 - beta_two) * rot_grad * rot_grad
    rot_step = rot_moment / (jnp.sqrt(new_second) + adam_eps)
    band_width = right_basis.shape[1]
    band_start = lax.axis_index("mp") * band_width
    grad_band = lax.dynamic_slice_in_dim(grad_full, band_start, band_width, 0)
    grad_strip = lax.dynamic_slice_in_dim(grad_full, band_start, band_width, 1)
    left_outer = lax.dot_general(grad_band, grad_full, (((1,), (1,)), ((), ())), precision=highest)
    right_outer = lax.dot_general(
        grad_strip, grad_full, (((0,), (0,)), ((), ())), precision=highest
    )
    new_left_stat = beta_stat * left_stat + (1.0 - beta_stat) * left_outer
    new_right_stat = beta_stat * right_stat + (1.0 - beta_stat) * right_outer
    order_count = left_stat.shape[1]
    stat_rows = jnp.stack([new_left_stat, new_right_stat]).astype(jnp.bfloat16)
    rot_step, stat_rows = lax.optimization_barrier((rot_step, stat_rows))
    stat_whole = lax.all_gather(stat_rows, "mp", axis=1, tiled=True)
    back_half = scatter_sum(
        lax.dot_general(right_basis, rot_step, (((1,), (1,)), ((), ())), precision=highest),
        "mp",
    )
    step_piece = scatter_sum(
        lax.dot_general(left_basis, back_half, (((1,), (1,)), ((), ())), precision=highest),
        "dp",
    )
    new_master = master - learn_rate * step_piece
    weights_block = gather_rows(new_master.astype(jnp.bfloat16), "dp").reshape(
        -1, new_master.shape[1]
    )
    new_bases = []
    for stat_part, basis_part in zip(stat_whole, (left_full, right_full)):
        power_part = jnp.dot(
            stat_part, basis_part.astype(jnp.bfloat16), preferred_element_type=jnp.float32
        )
        total = jnp.sum(power_part * power_part)
        whole_part = lax.optimization_barrier(
            (power_part * lax.rsqrt(total * (4.0 / order_count) + norm_eps)).astype(jnp.bfloat16)
        )
        gram = lax.optimization_barrier(row_gram(whole_part, whole_part).astype(jnp.bfloat16))
        square = jnp.dot(gram, gram, preferred_element_type=jnp.float32)
        poly = (quint_b * gram.astype(jnp.float32) + quint_c * square).astype(jnp.bfloat16)
        middle = quint_a * whole_part.astype(jnp.float32) + jnp.dot(
            poly, whole_part, preferred_element_type=jnp.float32
        )
        middle = lax.optimization_barrier(middle.astype(jnp.bfloat16))
        middle_rows = lax.dynamic_slice_in_dim(middle, band_start, band_width, 0)
        gram_two = row_gram(middle_rows, middle).astype(jnp.bfloat16)
        new_bases.append(
            1.5 * middle_rows.astype(jnp.float32)
            - 0.5 * jnp.dot(gram_two, middle, preferred_element_type=jnp.float32)
        )
    return (
        weights_block,
        new_master,
        new_moment,
        new_second,
        new_left_stat,
        new_right_stat,
        new_bases[0],
        new_bases[1],
    )


def solution(mesh):
    in_specs = (
        P("dp", None, None, "mp"),
        P("dp", "mp"),
        P("dp", "mp"),
        P("dp", "mp"),
        P(None, "dp"),
        P(None, "mp"),
        P("mp", None),
        P("mp", None),
    )
    out_specs = (
        P(None, "mp"),
        P("dp", "mp"),
        P("dp", "mp"),
        P("dp", "mp"),
        P("mp", None),
        P("mp", None),
        P("mp", None),
        P("mp", None),
    )
    return jax.shard_map(
        per_device, mesh=mesh, in_specs=in_specs, out_specs=out_specs, check_vma=False
    )
```

```python
import jax
import jax.numpy as jnp
from jax import lax
from jax.sharding import PartitionSpec as P

beta_one = 0.9
beta_two = 0.95
beta_stat = 0.95
learn_rate = 0.02
adam_eps = 1e-08
norm_eps = 1e-06
quint_a = 1.875
quint_b = -1.25
quint_c = 0.375
highest = lax.Precision.HIGH


def row_gram(row_part, whole_part):
    return lax.dot_general(
        row_part, whole_part, (((1,), (1,)), ((), ())), preferred_element_type=jnp.float32
    )


def scatter_sum(x, axis):
    count = lax.axis_size(axis)
    chunks = x.reshape((count, x.shape[0] // count) + x.shape[1:])
    return jnp.sum(lax.all_to_all(chunks, axis, 0, 0, tiled=False), axis=0)


def gather_rows(x, axis):
    count = lax.axis_size(axis)
    return lax.all_to_all(jnp.broadcast_to(x[None], (count,) + x.shape), axis, 0, 0, tiled=False)


def per_device(micro_grads, master, moment, second, left_basis, right_basis, left_stat, right_stat):
    dp_count = lax.axis_size("dp")
    micro_count = micro_grads.shape[1]
    local_sum = jnp.sum(micro_grads[0], axis=0, dtype=jnp.float32)
    grad_piece = scatter_sum(local_sum, "dp") / (micro_count * dp_count)
    new_moment = beta_one * moment + (1.0 - beta_one) * grad_piece
    pieces = gather_rows(jnp.stack([grad_piece, new_moment]), "dp")
    pieces = jnp.swapaxes(pieces, 0, 1).reshape(2, -1, pieces.shape[-1])
    left_cols = gather_rows(left_basis.astype(jnp.bfloat16), "dp")
    left_full = jnp.moveaxis(left_cols, 0, 1).reshape(left_basis.shape[0], -1)
    right_full = lax.all_gather(right_basis, "mp", axis=1, tiled=True)
    pieces, right_full = lax.optimization_barrier((pieces, right_full))
    both_full = lax.all_gather(pieces, "mp", axis=2, tiled=True)
    both_full, left_full = lax.optimization_barrier((both_full, left_full))
    grad_full = both_full[0]
    moment_full = both_full[1]

    def rotate(matrix):
        left_part = lax.dot_general(left_basis, matrix, (((0,), (0,)), ((), ())), precision=highest)
        return jnp.dot(left_part, right_basis, precision=highest)

    rot_grad = rotate(grad_full)
    rot_moment = rotate(moment_full)
    new_second = beta_two * second + (1.0 - beta_two) * rot_grad * rot_grad
    rot_step = rot_moment / (jnp.sqrt(new_second) + adam_eps)
    band_width = right_basis.shape[1]
    band_start = lax.axis_index("mp") * band_width
    grad_band = lax.dynamic_slice_in_dim(grad_full, band_start, band_width, 0)
    grad_strip = lax.dynamic_slice_in_dim(grad_full, band_start, band_width, 1)
    left_outer = lax.dot_general(grad_band, grad_full, (((1,), (1,)), ((), ())), precision=highest)
    right_outer = lax.dot_general(
        grad_strip, grad_full, (((0,), (0,)), ((), ())), precision=highest
    )
    new_left_stat = beta_stat * left_stat + (1.0 - beta_stat) * left_outer
    new_right_stat = beta_stat * right_stat + (1.0 - beta_stat) * right_outer
    order_count = left_stat.shape[1]
    stat_rows = jnp.stack([new_left_stat, new_right_stat]).astype(jnp.bfloat16)
    rot_step, stat_rows = lax.optimization_barrier((rot_step, stat_rows))
    stat_whole = lax.all_gather(stat_rows, "mp", axis=1, tiled=True)
    back_half = scatter_sum(
        lax.dot_general(right_basis, rot_step, (((1,), (1,)), ((), ())), precision=highest),
        "mp",
    )
    step_piece = scatter_sum(
        lax.dot_general(left_basis, back_half, (((1,), (1,)), ((), ())), precision=highest),
        "dp",
    )
    new_master = master - learn_rate * step_piece
    weights_block = gather_rows(new_master.astype(jnp.bfloat16), "dp").reshape(
        -1, new_master.shape[1]
    )
    new_bases = []
    for stat_part, basis_part in zip(stat_whole, (left_full, right_full)):
        power_part = jnp.dot(
            stat_part, basis_part.astype(jnp.bfloat16), preferred_element_type=jnp.float32
        )
        total = jnp.sum(power_part * power_part)
        whole_part = lax.optimization_barrier(
            (power_part * lax.rsqrt(total * (4.0 / order_count) + norm_eps)).astype(jnp.bfloat16)
        )
        gram = lax.optimization_barrier(row_gram(whole_part, whole_part).astype(jnp.bfloat16))
        square = jnp.dot(gram, gram, preferred_element_type=jnp.float32)
        poly = (quint_b * gram.astype(jnp.float32) + quint_c * square).astype(jnp.bfloat16)
        middle = quint_a * whole_part.astype(jnp.float32) + jnp.dot(
            poly, whole_part, preferred_element_type=jnp.float32
        )
        middle = lax.optimization_barrier(middle.astype(jnp.bfloat16))
        middle_rows = lax.dynamic_slice_in_dim(middle, band_start, band_width, 0)
        gram_two = row_gram(middle_rows, middle).astype(jnp.bfloat16)
        new_bases.append(
            1.5 * middle_rows.astype(jnp.float32)
            - 0.5 * jnp.dot(gram_two, middle, preferred_element_type=jnp.float32)
        )
    return (
        weights_block,
        new_master,
        new_moment,
        new_second,
        new_left_stat,
        new_right_stat,
        new_bases[0],
        new_bases[1],
    )


def solution(mesh):
    in_specs = (
        P("dp", None, None, "mp"),
        P("dp", "mp"),
        P("dp", "mp"),
        P("dp", "mp"),
        P(None, "dp"),
        P(None, "mp"),
        P("mp", None),
        P("mp", None),
    )
    out_specs = (
        P(None, "mp"),
        P("dp", "mp"),
        P("dp", "mp"),
        P("dp", "mp"),
        P("mp", None),
        P("mp", None),
        P("mp", None),
        P("mp", None),
    )
    return jax.shard_map(
        per_device, mesh=mesh, in_specs=in_specs, out_specs=out_specs, check_vma=False
    )
```

```python
import jax
import jax.numpy as jnp
from jax import lax
from jax.sharding import PartitionSpec as P

beta_one = 0.9
beta_two = 0.95
beta_stat = 0.95
learn_rate = 0.02
adam_eps = 1e-08
norm_eps = 1e-06
quint_a = 1.875
quint_b = -1.25
quint_c = 0.375
highest = lax.Precision.HIGH


def row_gram(row_part, whole_part):
    return lax.dot_general(
        row_part, whole_part, (((1,), (1,)), ((), ())), preferred_element_type=jnp.float32
    )


def scatter_sum(x, axis):
    count = lax.axis_size(axis)
    chunks = x.reshape((count, x.shape[0] // count) + x.shape[1:])
    return jnp.sum(lax.all_to_all(chunks, axis, 0, 0, tiled=False), axis=0)


def gather_rows(x, axis):
    count = lax.axis_size(axis)
    return lax.all_to_all(jnp.broadcast_to(x[None], (count,) + x.shape), axis, 0, 0, tiled=False)


def per_device(micro_grads, master, moment, second, left_basis, right_basis, left_stat, right_stat):
    dp_count = lax.axis_size("dp")
    micro_count = micro_grads.shape[1]
    local_sum = jnp.sum(micro_grads[0], axis=0, dtype=jnp.float32)
    grad_piece = scatter_sum(local_sum, "dp") / (micro_count * dp_count)
    new_moment = beta_one * moment + (1.0 - beta_one) * grad_piece
    moment_rows = gather_rows(moment, "mp")
    moment_rows = jnp.moveaxis(moment_rows, 0, 1).reshape(moment.shape[0], -1)
    moment_right = jnp.dot(moment_rows, right_basis, precision=highest)
    pieces = gather_rows(jnp.stack([grad_piece, moment_right]), "dp")
    pieces = jnp.swapaxes(pieces, 0, 1).reshape(2, -1, pieces.shape[-1])
    left_cols = gather_rows(left_basis.astype(jnp.bfloat16), "dp")
    left_full = jnp.moveaxis(left_cols, 0, 1).reshape(left_basis.shape[0], -1)
    right_full = lax.all_gather(right_basis, "mp", axis=1, tiled=True)
    pieces, right_full = lax.optimization_barrier((pieces, right_full))
    grad_full = lax.all_gather(pieces[0], "mp", axis=1, tiled=True)
    grad_full, left_full = lax.optimization_barrier((grad_full, left_full))
    moment_turned = lax.dot_general(
        left_basis, pieces[1], (((0,), (0,)), ((), ())), precision=highest
    )

    def rotate(matrix):
        left_part = lax.dot_general(left_basis, matrix, (((0,), (0,)), ((), ())), precision=highest)
        return jnp.dot(left_part, right_basis, precision=highest)

    rot_grad = rotate(grad_full)
    rot_moment = beta_one * moment_turned + (1.0 - beta_one) * rot_grad
    new_second = beta_two * second + (1.0 - beta_two) * rot_grad * rot_grad
    rot_step = rot_moment / (jnp.sqrt(new_second) + adam_eps)
    band_width = right_basis.shape[1]
    band_start = lax.axis_index("mp") * band_width
    grad_band = lax.dynamic_slice_in_dim(grad_full, band_start, band_width, 0)
    grad_strip = lax.dynamic_slice_in_dim(grad_full, band_start, band_width, 1)
    left_outer = lax.dot_general(grad_band, grad_full, (((1,), (1,)), ((), ())), precision=highest)
    right_outer = lax.dot_general(
        grad_strip, grad_full, (((0,), (0,)), ((), ())), precision=highest
    )
    new_left_stat = beta_stat * left_stat + (1.0 - beta_stat) * left_outer
    new_right_stat = beta_stat * right_stat + (1.0 - beta_stat) * right_outer
    order_count = left_stat.shape[1]
    stat_rows = jnp.stack([new_left_stat, new_right_stat]).astype(jnp.bfloat16)
    rot_step, stat_rows = lax.optimization_barrier((rot_step, stat_rows))
    stat_whole = lax.all_gather(stat_rows, "mp", axis=1, tiled=True)
    back_half = scatter_sum(
        lax.dot_general(right_basis, rot_step, (((1,), (1,)), ((), ())), precision=highest),
        "mp",
    )
    step_piece = scatter_sum(
        lax.dot_general(left_basis, back_half, (((1,), (1,)), ((), ())), precision=highest),
        "dp",
    )
    new_master = master - learn_rate * step_piece
    weights_block = gather_rows(new_master.astype(jnp.bfloat16), "dp").reshape(
        -1, new_master.shape[1]
    )
    new_bases = []
    for stat_part, basis_part in zip(stat_whole, (left_full, right_full)):
        power_part = jnp.dot(
            stat_part, basis_part.astype(jnp.bfloat16), preferred_element_type=jnp.float32
        )
        total = jnp.sum(power_part * power_part)
        whole_part = lax.optimization_barrier(
            (power_part * lax.rsqrt(total * (4.0 / order_count) + norm_eps)).astype(jnp.bfloat16)
        )
        gram = lax.optimization_barrier(row_gram(whole_part, whole_part).astype(jnp.bfloat16))
        square = jnp.dot(gram, gram, preferred_element_type=jnp.float32)
        poly = (quint_b * gram.astype(jnp.float32) + quint_c * square).astype(jnp.bfloat16)
        middle = quint_a * whole_part.astype(jnp.float32) + jnp.dot(
            poly, whole_part, preferred_element_type=jnp.float32
        )
        middle = lax.optimization_barrier(middle.astype(jnp.bfloat16))
        middle_rows = lax.dynamic_slice_in_dim(middle, band_start, band_width, 0)
        gram_two = row_gram(middle_rows, middle).astype(jnp.bfloat16)
        new_bases.append(
            1.5 * middle_rows.astype(jnp.float32)
            - 0.5 * jnp.dot(gram_two, middle, preferred_element_type=jnp.float32)
        )
    return (
        weights_block,
        new_master,
        new_moment,
        new_second,
        new_left_stat,
        new_right_stat,
        new_bases[0],
        new_bases[1],
    )


def solution(mesh):
    in_specs = (
        P("dp", None, None, "mp"),
        P("dp", "mp"),
        P("dp", "mp"),
        P("dp", "mp"),
        P(None, "dp"),
        P(None, "mp"),
        P("mp", None),
        P("mp", None),
    )
    out_specs = (
        P(None, "mp"),
        P("dp", "mp"),
        P("dp", "mp"),
        P("dp", "mp"),
        P("mp", None),
        P("mp", None),
        P("mp", None),
        P("mp", None),
    )
    return jax.shard_map(
        per_device, mesh=mesh, in_specs=in_specs, out_specs=out_specs, check_vma=False
    )
```

```python
import jax
import jax.numpy as jnp
from jax import lax
from jax.sharding import PartitionSpec as P

beta_one = 0.9
beta_two = 0.95
beta_stat = 0.95
learn_rate = 0.02
adam_eps = 1e-08
norm_eps = 1e-06
quint_a = 1.875
quint_b = -1.25
quint_c = 0.375
highest = lax.Precision.HIGH


def row_gram(row_part, whole_part):
    return lax.dot_general(
        row_part, whole_part, (((1,), (1,)), ((), ())), preferred_element_type=jnp.float32
    )


def scatter_sum(x, axis):
    count = lax.axis_size(axis)
    chunks = x.reshape((count, x.shape[0] // count) + x.shape[1:])
    return jnp.sum(lax.all_to_all(chunks, axis, 0, 0, tiled=False), axis=0)


def gather_rows(x, axis):
    count = lax.axis_size(axis)
    return lax.all_to_all(jnp.broadcast_to(x[None], (count,) + x.shape), axis, 0, 0, tiled=False)


def per_device(micro_grads, master, moment, second, left_basis, right_basis, left_stat, right_stat):
    dp_count = lax.axis_size("dp")
    micro_count = micro_grads.shape[1]
    local_sum = jnp.sum(micro_grads[0], axis=0, dtype=jnp.float32)
    grad_piece = scatter_sum(local_sum, "dp") / (micro_count * dp_count)
    new_moment = beta_one * moment + (1.0 - beta_one) * grad_piece
    moment_rows = lax.all_gather(moment, "mp", axis=1, tiled=True)
    moment_right = jnp.dot(moment_rows, right_basis, precision=highest)
    pieces = gather_rows(jnp.stack([grad_piece, moment_right]), "dp")
    pieces = jnp.swapaxes(pieces, 0, 1).reshape(2, -1, pieces.shape[-1])
    left_cols = gather_rows(left_basis.astype(jnp.bfloat16), "dp")
    left_full = jnp.moveaxis(left_cols, 0, 1).reshape(left_basis.shape[0], -1)
    right_full = lax.all_gather(right_basis, "mp", axis=1, tiled=True)
    pieces, right_full = lax.optimization_barrier((pieces, right_full))
    grad_full = lax.all_gather(pieces[0], "mp", axis=1, tiled=True)
    grad_full, left_full = lax.optimization_barrier((grad_full, left_full))
    moment_turned = lax.dot_general(
        left_basis, pieces[1], (((0,), (0,)), ((), ())), precision=highest
    )

    def rotate(matrix):
        left_part = lax.dot_general(left_basis, matrix, (((0,), (0,)), ((), ())), precision=highest)
        return jnp.dot(left_part, right_basis, precision=highest)

    rot_grad = rotate(grad_full)
    rot_moment = beta_one * moment_turned + (1.0 - beta_one) * rot_grad
    new_second = beta_two * second + (1.0 - beta_two) * rot_grad * rot_grad
    rot_step = rot_moment / (jnp.sqrt(new_second) + adam_eps)
    band_width = right_basis.shape[1]
    band_start = lax.axis_index("mp") * band_width
    grad_band = lax.dynamic_slice_in_dim(grad_full, band_start, band_width, 0)
    grad_strip = lax.dynamic_slice_in_dim(grad_full, band_start, band_width, 1)
    left_outer = lax.dot_general(grad_band, grad_full, (((1,), (1,)), ((), ())), precision=highest)
    right_outer = lax.dot_general(
        grad_strip, grad_full, (((0,), (0,)), ((), ())), precision=highest
    )
    new_left_stat = beta_stat * left_stat + (1.0 - beta_stat) * left_outer
    new_right_stat = beta_stat * right_stat + (1.0 - beta_stat) * right_outer
    order_count = left_stat.shape[1]
    stat_rows = jnp.stack([new_left_stat, new_right_stat]).astype(jnp.bfloat16)
    rot_step, stat_rows = lax.optimization_barrier((rot_step, stat_rows))
    stat_whole = lax.all_gather(stat_rows, "mp", axis=1, tiled=True)
    back_half = scatter_sum(
        lax.dot_general(right_basis, rot_step, (((1,), (1,)), ((), ())), precision=highest),
        "mp",
    )
    step_piece = scatter_sum(
        lax.dot_general(left_basis, back_half, (((1,), (1,)), ((), ())), precision=highest),
        "dp",
    )
    new_master = master - learn_rate * step_piece
    weights_block = gather_rows(new_master.astype(jnp.bfloat16), "dp").reshape(
        -1, new_master.shape[1]
    )
    new_bases = []
    for stat_part, basis_part in zip(stat_whole, (left_full, right_full)):
        power_part = jnp.dot(
            stat_part, basis_part.astype(jnp.bfloat16), preferred_element_type=jnp.float32
        )
        total = jnp.sum(power_part * power_part)
        whole_part = lax.optimization_barrier(
            (power_part * lax.rsqrt(total * (4.0 / order_count) + norm_eps)).astype(jnp.bfloat16)
        )
        gram = lax.optimization_barrier(row_gram(whole_part, whole_part).astype(jnp.bfloat16))
        square = jnp.dot(gram, gram, preferred_element_type=jnp.float32)
        poly = (quint_b * gram.astype(jnp.float32) + quint_c * square).astype(jnp.bfloat16)
        middle = quint_a * whole_part.astype(jnp.float32) + jnp.dot(
            poly, whole_part, preferred_element_type=jnp.float32
        )
        middle = lax.optimization_barrier(middle.astype(jnp.bfloat16))
        middle_rows = lax.dynamic_slice_in_dim(middle, band_start, band_width, 0)
        gram_two = row_gram(middle_rows, middle).astype(jnp.bfloat16)
        new_bases.append(
            1.5 * middle_rows.astype(jnp.float32)
            - 0.5 * jnp.dot(gram_two, middle, preferred_element_type=jnp.float32)
        )
    return (
        weights_block,
        new_master,
        new_moment,
        new_second,
        new_left_stat,
        new_right_stat,
        new_bases[0],
        new_bases[1],
    )


def solution(mesh):
    in_specs = (
        P("dp", None, None, "mp"),
        P("dp", "mp"),
        P("dp", "mp"),
        P("dp", "mp"),
        P(None, "dp"),
        P(None, "mp"),
        P("mp", None),
        P("mp", None),
    )
    out_specs = (
        P(None, "mp"),
        P("dp", "mp"),
        P("dp", "mp"),
        P("dp", "mp"),
        P("mp", None),
        P("mp", None),
        P("mp", None),
        P("mp", None),
    )
    return jax.shard_map(
        per_device, mesh=mesh, in_specs=in_specs, out_specs=out_specs, check_vma=False
    )
```

```python
import jax
import jax.numpy as jnp
from jax import lax
from jax.sharding import PartitionSpec as P

beta_one = 0.9
beta_two = 0.95
beta_stat = 0.95
learn_rate = 0.02
adam_eps = 1e-08
norm_eps = 1e-06
quint_a = 1.875
quint_b = -1.25
quint_c = 0.375
highest = lax.Precision.HIGH


def row_gram(row_part, whole_part):
    return lax.dot_general(
        row_part, whole_part, (((1,), (1,)), ((), ())), preferred_element_type=jnp.float32
    )


def scatter_sum(x, axis):
    count = lax.axis_size(axis)
    chunks = x.reshape((count, x.shape[0] // count) + x.shape[1:])
    return jnp.sum(lax.all_to_all(chunks, axis, 0, 0, tiled=False), axis=0)


def gather_rows(x, axis):
    count = lax.axis_size(axis)
    return lax.all_to_all(jnp.broadcast_to(x[None], (count,) + x.shape), axis, 0, 0, tiled=False)


def doubling_gather(x, axis):
    count = lax.axis_size(axis)
    index = lax.axis_index(axis)
    parts = x[None]
    step = 1
    while step < count:
        other = lax.ppermute(parts, axis, [(i, i ^ step) for i in range(count)])
        lower = (index // step) % 2 == 0
        parts = jnp.concatenate(
            [jnp.where(lower, parts, other), jnp.where(lower, other, parts)], axis=0
        )
        step *= 2
    return parts


def per_device(micro_grads, master, moment, second, left_basis, right_basis, left_stat, right_stat):
    dp_count = lax.axis_size("dp")
    micro_count = micro_grads.shape[1]
    local_sum = jnp.sum(micro_grads[0], axis=0, dtype=jnp.float32)
    grad_piece = scatter_sum(local_sum, "dp") / (micro_count * dp_count)
    new_moment = beta_one * moment + (1.0 - beta_one) * grad_piece
    moment_rows = gather_rows(moment, "mp")
    moment_rows = jnp.moveaxis(moment_rows, 0, 1).reshape(moment.shape[0], -1)
    moment_right = jnp.dot(moment_rows, right_basis, precision=highest)
    pieces = gather_rows(jnp.stack([grad_piece, moment_right]), "dp")
    pieces = jnp.swapaxes(pieces, 0, 1).reshape(2, -1, pieces.shape[-1])
    left_cols = doubling_gather(left_basis.astype(jnp.bfloat16), "dp")
    left_full = jnp.moveaxis(left_cols, 0, 1).reshape(left_basis.shape[0], -1)
    right_full = lax.all_gather(right_basis, "mp", axis=1, tiled=True)
    pieces, right_full = lax.optimization_barrier((pieces, right_full))
    grad_full = lax.all_gather(pieces[0], "mp", axis=1, tiled=True)
    moment_turned = lax.dot_general(
        left_basis, pieces[1], (((0,), (0,)), ((), ())), precision=highest
    )

    def rotate(matrix):
        left_part = lax.dot_general(left_basis, matrix, (((0,), (0,)), ((), ())), precision=highest)
        return jnp.dot(left_part, right_basis, precision=highest)

    rot_grad = rotate(grad_full)
    rot_moment = beta_one * moment_turned + (1.0 - beta_one) * rot_grad
    new_second = beta_two * second + (1.0 - beta_two) * rot_grad * rot_grad
    rot_step = rot_moment / (jnp.sqrt(new_second) + adam_eps)
    band_width = right_basis.shape[1]
    band_start = lax.axis_index("mp") * band_width
    grad_band = lax.dynamic_slice_in_dim(grad_full, band_start, band_width, 0)
    grad_strip = lax.dynamic_slice_in_dim(grad_full, band_start, band_width, 1)
    left_outer = lax.dot_general(grad_band, grad_full, (((1,), (1,)), ((), ())), precision=highest)
    right_outer = lax.dot_general(
        grad_strip, grad_full, (((0,), (0,)), ((), ())), precision=highest
    )
    new_left_stat = beta_stat * left_stat + (1.0 - beta_stat) * left_outer
    new_right_stat = beta_stat * right_stat + (1.0 - beta_stat) * right_outer
    order_count = left_stat.shape[1]
    stat_rows = jnp.stack([new_left_stat, new_right_stat]).astype(jnp.bfloat16)
    rot_step, stat_rows = lax.optimization_barrier((rot_step, stat_rows))
    stat_whole = lax.all_gather(stat_rows, "mp", axis=1, tiled=True)
    back_half = scatter_sum(
        lax.dot_general(right_basis, rot_step, (((1,), (1,)), ((), ())), precision=highest),
        "mp",
    )
    step_piece = scatter_sum(
        lax.dot_general(left_basis, back_half, (((1,), (1,)), ((), ())), precision=highest),
        "dp",
    )
    new_master = master - learn_rate * step_piece
    weights_block = gather_rows(new_master.astype(jnp.bfloat16), "dp").reshape(
        -1, new_master.shape[1]
    )
    new_bases = []
    for stat_part, basis_part in zip(stat_whole, (left_full, right_full)):
        power_part = jnp.dot(
            stat_part, basis_part.astype(jnp.bfloat16), preferred_element_type=jnp.float32
        )
        total = jnp.sum(power_part * power_part)
        whole_part = lax.optimization_barrier(
            (power_part * lax.rsqrt(total * (4.0 / order_count) + norm_eps)).astype(jnp.bfloat16)
        )
        gram = lax.optimization_barrier(row_gram(whole_part, whole_part).astype(jnp.bfloat16))
        square = jnp.dot(gram, gram, preferred_element_type=jnp.float32)
        poly = (quint_b * gram.astype(jnp.float32) + quint_c * square).astype(jnp.bfloat16)
        middle = quint_a * whole_part.astype(jnp.float32) + jnp.dot(
            poly, whole_part, preferred_element_type=jnp.float32
        )
        middle = lax.optimization_barrier(middle.astype(jnp.bfloat16))
        middle_rows = lax.dynamic_slice_in_dim(middle, band_start, band_width, 0)
        gram_two = row_gram(middle_rows, middle).astype(jnp.bfloat16)
        new_bases.append(
            1.5 * middle_rows.astype(jnp.float32)
            - 0.5 * jnp.dot(gram_two, middle, preferred_element_type=jnp.float32)
        )
    return (
        weights_block,
        new_master,
        new_moment,
        new_second,
        new_left_stat,
        new_right_stat,
        new_bases[0],
        new_bases[1],
    )


def solution(mesh):
    in_specs = (
        P("dp", None, None, "mp"),
        P("dp", "mp"),
        P("dp", "mp"),
        P("dp", "mp"),
        P(None, "dp"),
        P(None, "mp"),
        P("mp", None),
        P("mp", None),
    )
    out_specs = (
        P(None, "mp"),
        P("dp", "mp"),
        P("dp", "mp"),
        P("dp", "mp"),
        P("mp", None),
        P("mp", None),
        P("mp", None),
        P("mp", None),
    )
    return jax.shard_map(
        per_device, mesh=mesh, in_specs=in_specs, out_specs=out_specs, check_vma=False
    )
```

```python
import jax
import jax.numpy as jnp
from jax import lax
from jax.sharding import PartitionSpec as P

beta_one = 0.9
beta_two = 0.95
beta_stat = 0.95
learn_rate = 0.02
adam_eps = 1e-08
norm_eps = 1e-06
quint_a = 1.875
quint_b = -1.25
quint_c = 0.375
highest = lax.Precision.HIGH


def row_gram(row_part, whole_part):
    return lax.dot_general(
        row_part, whole_part, (((1,), (1,)), ((), ())), preferred_element_type=jnp.float32
    )


def scatter_sum(x, axis):
    count = lax.axis_size(axis)
    chunks = x.reshape(count, -1)
    summed = jnp.sum(lax.all_to_all(chunks, axis, 0, 0, tiled=False), axis=0)
    return summed.reshape((x.shape[0] // count,) + x.shape[1:])


def gather_rows(x, axis):
    count = lax.axis_size(axis)
    flat = jnp.broadcast_to(x.reshape(1, -1), (count, x.size))
    return lax.all_to_all(flat, axis, 0, 0, tiled=False).reshape((count,) + x.shape)


def per_device(micro_grads, master, moment, second, left_basis, right_basis, left_stat, right_stat):
    dp_count = lax.axis_size("dp")
    micro_count = micro_grads.shape[1]
    local_sum = jnp.sum(micro_grads[0], axis=0, dtype=jnp.float32)
    grad_piece = scatter_sum(local_sum, "dp") / (micro_count * dp_count)
    new_moment = beta_one * moment + (1.0 - beta_one) * grad_piece
    moment_rows = gather_rows(moment, "mp")
    moment_rows = jnp.moveaxis(moment_rows, 0, 1).reshape(moment.shape[0], -1)
    moment_right = jnp.dot(moment_rows, right_basis, precision=highest)
    pieces = gather_rows(jnp.stack([grad_piece, moment_right]), "dp")
    pieces = jnp.swapaxes(pieces, 0, 1).reshape(2, -1, pieces.shape[-1])
    left_cols = gather_rows(left_basis.astype(jnp.bfloat16), "dp")
    left_full = jnp.moveaxis(left_cols, 0, 1).reshape(left_basis.shape[0], -1)
    right_full = lax.all_gather(right_basis, "mp", axis=1, tiled=True)
    pieces, right_full = lax.optimization_barrier((pieces, right_full))
    grad_full = lax.all_gather(pieces[0], "mp", axis=1, tiled=True)
    grad_full, left_full = lax.optimization_barrier((grad_full, left_full))
    moment_turned = lax.dot_general(
        left_basis, pieces[1], (((0,), (0,)), ((), ())), precision=highest
    )

    def rotate(matrix):
        left_part = lax.dot_general(left_basis, matrix, (((0,), (0,)), ((), ())), precision=highest)
        return jnp.dot(left_part, right_basis, precision=highest)

    rot_grad = rotate(grad_full)
    rot_moment = beta_one * moment_turned + (1.0 - beta_one) * rot_grad
    new_second = beta_two * second + (1.0 - beta_two) * rot_grad * rot_grad
    rot_step = rot_moment / (jnp.sqrt(new_second) + adam_eps)
    band_width = right_basis.shape[1]
    band_start = lax.axis_index("mp") * band_width
    grad_band = lax.dynamic_slice_in_dim(grad_full, band_start, band_width, 0)
    grad_strip = lax.dynamic_slice_in_dim(grad_full, band_start, band_width, 1)
    left_outer = lax.dot_general(grad_band, grad_full, (((1,), (1,)), ((), ())), precision=highest)
    right_outer = lax.dot_general(
        grad_strip, grad_full, (((0,), (0,)), ((), ())), precision=highest
    )
    new_left_stat = beta_stat * left_stat + (1.0 - beta_stat) * left_outer
    new_right_stat = beta_stat * right_stat + (1.0 - beta_stat) * right_outer
    order_count = left_stat.shape[1]
    stat_rows = jnp.stack([new_left_stat, new_right_stat]).astype(jnp.bfloat16)
    rot_step, stat_rows = lax.optimization_barrier((rot_step, stat_rows))
    stat_whole = lax.all_gather(stat_rows, "mp", axis=1, tiled=True)
    back_half = scatter_sum(
        lax.dot_general(right_basis, rot_step, (((1,), (1,)), ((), ())), precision=highest),
        "mp",
    )
    step_piece = scatter_sum(
        lax.dot_general(left_basis, back_half, (((1,), (1,)), ((), ())), precision=highest),
        "dp",
    )
    new_master = master - learn_rate * step_piece
    weights_block = gather_rows(new_master.astype(jnp.bfloat16), "dp").reshape(
        -1, new_master.shape[1]
    )
    new_bases = []
    for stat_part, basis_part in zip(stat_whole, (left_full, right_full)):
        power_part = jnp.dot(
            stat_part, basis_part.astype(jnp.bfloat16), preferred_element_type=jnp.float32
        )
        total = jnp.sum(power_part * power_part)
        whole_part = lax.optimization_barrier(
            (power_part * lax.rsqrt(total * (4.0 / order_count) + norm_eps)).astype(jnp.bfloat16)
        )
        gram = lax.optimization_barrier(row_gram(whole_part, whole_part).astype(jnp.bfloat16))
        square = jnp.dot(gram, gram, preferred_element_type=jnp.float32)
        poly = (quint_b * gram.astype(jnp.float32) + quint_c * square).astype(jnp.bfloat16)
        middle = quint_a * whole_part.astype(jnp.float32) + jnp.dot(
            poly, whole_part, preferred_element_type=jnp.float32
        )
        middle = lax.optimization_barrier(middle.astype(jnp.bfloat16))
        middle_rows = lax.dynamic_slice_in_dim(middle, band_start, band_width, 0)
        gram_two = row_gram(middle_rows, middle).astype(jnp.bfloat16)
        new_bases.append(
            1.5 * middle_rows.astype(jnp.float32)
            - 0.5 * jnp.dot(gram_two, middle, preferred_element_type=jnp.float32)
        )
    return (
        weights_block,
        new_master,
        new_moment,
        new_second,
        new_left_stat,
        new_right_stat,
        new_bases[0],
        new_bases[1],
    )


def solution(mesh):
    in_specs = (
        P("dp", None, None, "mp"),
        P("dp", "mp"),
        P("dp", "mp"),
        P("dp", "mp"),
        P(None, "dp"),
        P(None, "mp"),
        P("mp", None),
        P("mp", None),
    )
    out_specs = (
        P(None, "mp"),
        P("dp", "mp"),
        P("dp", "mp"),
        P("dp", "mp"),
        P("mp", None),
        P("mp", None),
        P("mp", None),
        P("mp", None),
    )
    return jax.shard_map(
        per_device, mesh=mesh, in_specs=in_specs, out_specs=out_specs, check_vma=False
    )
```

```python
import jax
import jax.numpy as jnp
from jax import lax
from jax.sharding import PartitionSpec as P

beta_one = 0.9
beta_two = 0.95
beta_stat = 0.95
learn_rate = 0.02
adam_eps = 1e-08
norm_eps = 1e-06
quint_a = 1.875
quint_b = -1.25
quint_c = 0.375
highest = lax.Precision.HIGH


def row_gram(row_part, whole_part):
    return lax.dot_general(
        row_part, whole_part, (((1,), (1,)), ((), ())), preferred_element_type=jnp.float32
    )


def scatter_sum(x, axis):
    count = lax.axis_size(axis)
    chunks = x.reshape((count, x.shape[0] // count) + x.shape[1:])
    return jnp.sum(lax.all_to_all(chunks, axis, 0, 0, tiled=False), axis=0)


def gather_rows(x, axis):
    count = lax.axis_size(axis)
    return lax.all_to_all(jnp.broadcast_to(x[None], (count,) + x.shape), axis, 0, 0, tiled=False)


def per_device(micro_grads, master, moment, second, left_basis, right_basis, left_stat, right_stat):
    dp_count = lax.axis_size("dp")
    micro_count = micro_grads.shape[1]
    local_sum = jnp.sum(micro_grads[0], axis=0, dtype=jnp.float32)
    grad_piece = scatter_sum(local_sum, "dp") / (micro_count * dp_count)
    new_moment = beta_one * moment + (1.0 - beta_one) * grad_piece
    moment_rows = gather_rows(moment, "mp")
    moment_rows = jnp.moveaxis(moment_rows, 0, 1).reshape(moment.shape[0], -1)
    moment_right = jnp.dot(moment_rows, right_basis, precision=highest)
    pieces = gather_rows(jnp.stack([grad_piece, moment_right]), "dp")
    pieces = jnp.swapaxes(pieces, 0, 1).reshape(2, -1, pieces.shape[-1])
    left_cols = gather_rows(left_basis.astype(jnp.bfloat16), "dp")
    left_full = jnp.moveaxis(left_cols, 0, 1).reshape(left_basis.shape[0], -1)
    right_full = lax.all_gather(right_basis, "mp", axis=1, tiled=True)
    pieces, right_full = lax.optimization_barrier((pieces, right_full))
    grad_full = lax.all_gather(pieces[0], "mp", axis=1, tiled=True)
    grad_full, left_full = lax.optimization_barrier((grad_full, left_full))
    moment_turned = lax.dot_general(
        left_basis, pieces[1], (((0,), (0,)), ((), ())), precision=highest
    )

    def rotate(matrix):
        left_part = lax.dot_general(left_basis, matrix, (((0,), (0,)), ((), ())), precision=highest)
        return jnp.dot(left_part, right_basis, precision=highest)

    rot_grad = rotate(grad_full)
    rot_moment = beta_one * moment_turned + (1.0 - beta_one) * rot_grad
    new_second = beta_two * second + (1.0 - beta_two) * rot_grad * rot_grad
    rot_step = rot_moment / (jnp.sqrt(new_second) + adam_eps)
    band_width = right_basis.shape[1]
    band_start = lax.axis_index("mp") * band_width
    grad_band = lax.dynamic_slice_in_dim(grad_full, band_start, band_width, 0)
    grad_strip = lax.dynamic_slice_in_dim(grad_full, band_start, band_width, 1)
    left_outer = lax.dot_general(grad_band, grad_full, (((1,), (1,)), ((), ())), precision=highest)
    right_outer = lax.dot_general(
        grad_strip, grad_full, (((0,), (0,)), ((), ())), precision=highest
    )
    new_left_stat = beta_stat * left_stat + (1.0 - beta_stat) * left_outer
    new_right_stat = beta_stat * right_stat + (1.0 - beta_stat) * right_outer
    order_count = left_stat.shape[1]
    stat_rows = jnp.stack([new_left_stat, new_right_stat]).astype(jnp.bfloat16)
    rot_step, stat_rows = lax.optimization_barrier((rot_step, stat_rows))
    stat_whole = lax.all_gather(stat_rows, "mp", axis=1, tiled=True)
    back_half = scatter_sum(
        lax.dot_general(right_basis, rot_step, (((1,), (1,)), ((), ())), precision=highest),
        "mp",
    )
    step_piece = scatter_sum(
        lax.dot_general(left_basis, back_half, (((1,), (1,)), ((), ())), precision=highest),
        "dp",
    )
    new_master = master - learn_rate * step_piece
    weights_block = gather_rows(new_master.astype(jnp.bfloat16), "dp").reshape(
        -1, new_master.shape[1]
    )
    basis_whole = jnp.stack([left_full.astype(jnp.bfloat16), right_full.astype(jnp.bfloat16)])
    power = jnp.einsum("sij,sjk->sik", stat_whole, basis_whole, preferred_element_type=jnp.float32)
    total = jnp.sum(power * power, axis=(1, 2), keepdims=True)
    start = lax.optimization_barrier(
        (power * lax.rsqrt(total * (4.0 / order_count) + norm_eps)).astype(jnp.bfloat16)
    )
    gram = lax.optimization_barrier(
        jnp.einsum("sij,skj->sik", start, start, preferred_element_type=jnp.float32).astype(
            jnp.bfloat16
        )
    )
    square = jnp.einsum("sij,sjk->sik", gram, gram, preferred_element_type=jnp.float32)
    poly = (quint_b * gram.astype(jnp.float32) + quint_c * square).astype(jnp.bfloat16)
    middle = quint_a * start.astype(jnp.float32) + jnp.einsum(
        "sij,sjk->sik", poly, start, preferred_element_type=jnp.float32
    )
    middle = lax.optimization_barrier(middle.astype(jnp.bfloat16))
    middle_rows = lax.dynamic_slice_in_dim(middle, band_start, band_width, 1)
    gram_two = jnp.einsum(
        "sij,skj->sik", middle_rows, middle, preferred_element_type=jnp.float32
    ).astype(jnp.bfloat16)
    new_bases = 1.5 * middle_rows.astype(jnp.float32) - 0.5 * jnp.einsum(
        "sij,sjk->sik", gram_two, middle, preferred_element_type=jnp.float32
    )
    return (
        weights_block,
        new_master,
        new_moment,
        new_second,
        new_left_stat,
        new_right_stat,
        new_bases[0],
        new_bases[1],
    )


def solution(mesh):
    in_specs = (
        P("dp", None, None, "mp"),
        P("dp", "mp"),
        P("dp", "mp"),
        P("dp", "mp"),
        P(None, "dp"),
        P(None, "mp"),
        P("mp", None),
        P("mp", None),
    )
    out_specs = (
        P(None, "mp"),
        P("dp", "mp"),
        P("dp", "mp"),
        P("dp", "mp"),
        P("mp", None),
        P("mp", None),
        P("mp", None),
        P("mp", None),
    )
    return jax.shard_map(
        per_device, mesh=mesh, in_specs=in_specs, out_specs=out_specs, check_vma=False
    )
```

```python
import jax
import jax.numpy as jnp
from jax import lax
from jax.sharding import PartitionSpec as P

beta_one = 0.9
beta_two = 0.95
beta_stat = 0.95
learn_rate = 0.02
adam_eps = 1e-08
norm_eps = 1e-06
quint_a = 1.875
quint_b = -1.25
quint_c = 0.375
highest = lax.Precision.HIGH


def row_gram(row_part, whole_part):
    return lax.dot_general(
        row_part, whole_part, (((1,), (1,)), ((), ())), preferred_element_type=jnp.float32
    )


def scatter_sum(x, axis):
    count = lax.axis_size(axis)
    chunks = x.reshape((count, x.shape[0] // count) + x.shape[1:])
    return jnp.sum(lax.all_to_all(chunks, axis, 0, 0, tiled=False), axis=0)


def gather_rows(x, axis):
    count = lax.axis_size(axis)
    return lax.all_to_all(jnp.broadcast_to(x[None], (count,) + x.shape), axis, 0, 0, tiled=False)


def per_device(micro_grads, master, moment, second, left_basis, right_basis, left_stat, right_stat):
    dp_count = lax.axis_size("dp")
    micro_count = micro_grads.shape[1]
    local_sum = jnp.sum(micro_grads[0], axis=0, dtype=jnp.float32)
    grad_piece = scatter_sum(local_sum, "dp") / (micro_count * dp_count)
    new_moment = beta_one * moment + (1.0 - beta_one) * grad_piece
    pieces = gather_rows(jnp.stack([grad_piece, moment]), "dp")
    pieces = jnp.swapaxes(pieces, 0, 1).reshape(2, -1, pieces.shape[-1])
    left_cols = gather_rows(left_basis.astype(jnp.bfloat16), "dp")
    left_full = jnp.moveaxis(left_cols, 0, 1).reshape(left_basis.shape[0], -1)
    moment_left = lax.dot_general(
        left_basis, pieces[1], (((0,), (0,)), ((), ())), precision=highest
    )
    packed = jnp.concatenate([pieces[0], moment_left], axis=0)
    right_full = lax.all_gather(right_basis, "mp", axis=1, tiled=True)
    packed, right_full = lax.optimization_barrier((packed, right_full))
    gathered = lax.all_gather(packed, "mp", axis=1, tiled=True)
    grad_full = gathered[: pieces.shape[1]]
    grad_full, left_full = lax.optimization_barrier((grad_full, left_full))
    moment_turned = jnp.dot(gathered[pieces.shape[1] :], right_basis, precision=highest)

    def rotate(matrix):
        left_part = lax.dot_general(left_basis, matrix, (((0,), (0,)), ((), ())), precision=highest)
        return jnp.dot(left_part, right_basis, precision=highest)

    rot_grad = rotate(grad_full)
    rot_moment = beta_one * moment_turned + (1.0 - beta_one) * rot_grad
    new_second = beta_two * second + (1.0 - beta_two) * rot_grad * rot_grad
    rot_step = rot_moment / (jnp.sqrt(new_second) + adam_eps)
    band_width = right_basis.shape[1]
    band_start = lax.axis_index("mp") * band_width
    grad_band = lax.dynamic_slice_in_dim(grad_full, band_start, band_width, 0)
    grad_strip = lax.dynamic_slice_in_dim(grad_full, band_start, band_width, 1)
    left_outer = lax.dot_general(grad_band, grad_full, (((1,), (1,)), ((), ())), precision=highest)
    right_outer = lax.dot_general(
        grad_strip, grad_full, (((0,), (0,)), ((), ())), precision=highest
    )
    new_left_stat = beta_stat * left_stat + (1.0 - beta_stat) * left_outer
    new_right_stat = beta_stat * right_stat + (1.0 - beta_stat) * right_outer
    order_count = left_stat.shape[1]
    stat_rows = jnp.stack([new_left_stat, new_right_stat]).astype(jnp.bfloat16)
    rot_step, stat_rows = lax.optimization_barrier((rot_step, stat_rows))
    stat_whole = lax.all_gather(stat_rows, "mp", axis=1, tiled=True)
    back_half = scatter_sum(
        lax.dot_general(right_basis, rot_step, (((1,), (1,)), ((), ())), precision=highest),
        "mp",
    )
    step_piece = scatter_sum(
        lax.dot_general(left_basis, back_half, (((1,), (1,)), ((), ())), precision=highest),
        "dp",
    )
    new_master = master - learn_rate * step_piece
    weights_block = gather_rows(new_master.astype(jnp.bfloat16), "dp").reshape(
        -1, new_master.shape[1]
    )
    basis_whole = jnp.stack([left_full.astype(jnp.bfloat16), right_full.astype(jnp.bfloat16)])
    power = jnp.einsum("sij,sjk->sik", stat_whole, basis_whole, preferred_element_type=jnp.float32)
    total = jnp.sum(power * power, axis=(1, 2), keepdims=True)
    start = lax.optimization_barrier(
        (power * lax.rsqrt(total * (4.0 / order_count) + norm_eps)).astype(jnp.bfloat16)
    )
    gram = lax.optimization_barrier(
        jnp.einsum("sij,skj->sik", start, start, preferred_element_type=jnp.float32).astype(
            jnp.bfloat16
        )
    )
    square = jnp.einsum("sij,sjk->sik", gram, gram, preferred_element_type=jnp.float32)
    poly = (quint_b * gram.astype(jnp.float32) + quint_c * square).astype(jnp.bfloat16)
    middle = quint_a * start.astype(jnp.float32) + jnp.einsum(
        "sij,sjk->sik", poly, start, preferred_element_type=jnp.float32
    )
    middle = lax.optimization_barrier(middle.astype(jnp.bfloat16))
    middle_rows = lax.dynamic_slice_in_dim(middle, band_start, band_width, 1)
    gram_two = jnp.einsum(
        "sij,skj->sik", middle_rows, middle, preferred_element_type=jnp.float32
    ).astype(jnp.bfloat16)
    new_bases = 1.5 * middle_rows.astype(jnp.float32) - 0.5 * jnp.einsum(
        "sij,sjk->sik", gram_two, middle, preferred_element_type=jnp.float32
    )
    return (
        weights_block,
        new_master,
        new_moment,
        new_second,
        new_left_stat,
        new_right_stat,
        new_bases[0],
        new_bases[1],
    )


def solution(mesh):
    in_specs = (
        P("dp", None, None, "mp"),
        P("dp", "mp"),
        P("dp", "mp"),
        P("dp", "mp"),
        P(None, "dp"),
        P(None, "mp"),
        P("mp", None),
        P("mp", None),
    )
    out_specs = (
        P(None, "mp"),
        P("dp", "mp"),
        P("dp", "mp"),
        P("dp", "mp"),
        P("mp", None),
        P("mp", None),
        P("mp", None),
        P("mp", None),
    )
    return jax.shard_map(
        per_device, mesh=mesh, in_specs=in_specs, out_specs=out_specs, check_vma=False
    )
```

```python
import jax
import jax.numpy as jnp
from jax import lax
from jax.sharding import PartitionSpec as P

beta_one = 0.9
beta_two = 0.95
beta_stat = 0.95
learn_rate = 0.02
adam_eps = 1e-08
norm_eps = 1e-06
quint_a = 1.875
quint_b = -1.25
quint_c = 0.375
highest = lax.Precision.HIGH


def row_gram(row_part, whole_part):
    return lax.dot_general(
        row_part, whole_part, (((1,), (1,)), ((), ())), preferred_element_type=jnp.float32
    )


def scatter_sum(x, axis):
    count = lax.axis_size(axis)
    chunks = x.reshape((count, x.shape[0] // count) + x.shape[1:])
    return jnp.sum(lax.all_to_all(chunks, axis, 0, 0, tiled=False), axis=0)


def gather_rows(x, axis):
    count = lax.axis_size(axis)
    return lax.all_to_all(jnp.broadcast_to(x[None], (count,) + x.shape), axis, 0, 0, tiled=False)


def per_device(micro_grads, master, moment, second, left_basis, right_basis, left_stat, right_stat):
    dp_count = lax.axis_size("dp")
    micro_count = micro_grads.shape[1]
    local_sum = jnp.sum(micro_grads[0], axis=0, dtype=jnp.float32)
    grad_piece = scatter_sum(local_sum, "dp") / (micro_count * dp_count)
    new_moment = beta_one * moment + (1.0 - beta_one) * grad_piece
    pieces = gather_rows(jnp.stack([grad_piece, moment]), "dp")
    pieces = jnp.swapaxes(pieces, 0, 1).reshape(2, -1, pieces.shape[-1])
    left_cols = gather_rows(left_basis.astype(jnp.bfloat16), "dp")
    left_full = jnp.moveaxis(left_cols, 0, 1).reshape(left_basis.shape[0], -1)
    moment_left = lax.dot_general(
        left_basis, pieces[1], (((0,), (0,)), ((), ())), precision=highest
    )
    packed = jnp.concatenate([pieces[0], moment_left], axis=0)
    right_full = lax.all_gather(right_basis, "mp", axis=1, tiled=True)
    packed, right_full = lax.optimization_barrier((packed, right_full))
    gathered = lax.all_gather(packed, "mp", axis=1, tiled=True)
    grad_full = gathered[: pieces.shape[1]]
    grad_full, left_full = lax.optimization_barrier((grad_full, left_full))
    moment_turned = jnp.dot(gathered[pieces.shape[1] :], right_basis, precision=highest)

    def rotate(matrix):
        left_part = lax.dot_general(left_basis, matrix, (((0,), (0,)), ((), ())), precision=highest)
        return jnp.dot(left_part, right_basis, precision=highest)

    rot_grad = rotate(grad_full)
    rot_moment = beta_one * moment_turned + (1.0 - beta_one) * rot_grad
    new_second = beta_two * second + (1.0 - beta_two) * rot_grad * rot_grad
    rot_step = rot_moment / (jnp.sqrt(new_second) + adam_eps)
    band_width = right_basis.shape[1]
    band_start = lax.axis_index("mp") * band_width
    grad_band = lax.dynamic_slice_in_dim(grad_full, band_start, band_width, 0)
    grad_strip = lax.dynamic_slice_in_dim(grad_full, band_start, band_width, 1)
    left_outer = lax.dot_general(grad_band, grad_full, (((1,), (1,)), ((), ())), precision=highest)
    right_outer = lax.dot_general(
        grad_strip, grad_full, (((0,), (0,)), ((), ())), precision=highest
    )
    new_left_stat = beta_stat * left_stat + (1.0 - beta_stat) * left_outer
    new_right_stat = beta_stat * right_stat + (1.0 - beta_stat) * right_outer
    order_count = left_stat.shape[1]
    stat_rows = jnp.stack([new_left_stat, new_right_stat]).astype(jnp.bfloat16)
    rot_step, stat_rows = lax.optimization_barrier((rot_step, stat_rows))
    stat_whole = lax.all_gather(stat_rows, "mp", axis=1, tiled=True)
    back_half = scatter_sum(
        lax.dot_general(right_basis, rot_step, (((1,), (1,)), ((), ())), precision=highest),
        "mp",
    )
    step_piece = scatter_sum(
        lax.dot_general(left_basis, back_half, (((1,), (1,)), ((), ())), precision=highest),
        "dp",
    )
    new_master = master - learn_rate * step_piece
    weights_block = gather_rows(new_master.astype(jnp.bfloat16), "dp").reshape(
        -1, new_master.shape[1]
    )
    basis_whole = jnp.stack([left_full.astype(jnp.bfloat16), right_full.astype(jnp.bfloat16)])
    power = jnp.einsum("sij,sjk->sik", stat_whole, basis_whole, preferred_element_type=jnp.float32)
    total = jnp.sum(power * power, axis=(1, 2), keepdims=True)
    start = (power * lax.rsqrt(total * (4.0 / order_count) + norm_eps)).astype(jnp.bfloat16)
    gram = jnp.einsum("sij,skj->sik", start, start, preferred_element_type=jnp.float32).astype(
        jnp.bfloat16
    )
    square = jnp.einsum("sij,sjk->sik", gram, gram, preferred_element_type=jnp.float32)
    poly = (quint_b * gram.astype(jnp.float32) + quint_c * square).astype(jnp.bfloat16)
    middle = quint_a * start.astype(jnp.float32) + jnp.einsum(
        "sij,sjk->sik", poly, start, preferred_element_type=jnp.float32
    )
    middle = middle.astype(jnp.bfloat16)
    middle_rows = lax.dynamic_slice_in_dim(middle, band_start, band_width, 1)
    gram_two = jnp.einsum(
        "sij,skj->sik", middle_rows, middle, preferred_element_type=jnp.float32
    ).astype(jnp.bfloat16)
    new_bases = 1.5 * middle_rows.astype(jnp.float32) - 0.5 * jnp.einsum(
        "sij,sjk->sik", gram_two, middle, preferred_element_type=jnp.float32
    )
    return (
        weights_block,
        new_master,
        new_moment,
        new_second,
        new_left_stat,
        new_right_stat,
        new_bases[0],
        new_bases[1],
    )


def solution(mesh):
    in_specs = (
        P("dp", None, None, "mp"),
        P("dp", "mp"),
        P("dp", "mp"),
        P("dp", "mp"),
        P(None, "dp"),
        P(None, "mp"),
        P("mp", None),
        P("mp", None),
    )
    out_specs = (
        P(None, "mp"),
        P("dp", "mp"),
        P("dp", "mp"),
        P("dp", "mp"),
        P("mp", None),
        P("mp", None),
        P("mp", None),
        P("mp", None),
    )
    return jax.shard_map(
        per_device, mesh=mesh, in_specs=in_specs, out_specs=out_specs, check_vma=False
    )
```

```python
import jax
import jax.numpy as jnp
from jax import lax
from jax.sharding import PartitionSpec as P

beta_one = 0.9
beta_two = 0.95
beta_stat = 0.95
learn_rate = 0.02
adam_eps = 1e-08
norm_eps = 1e-06
quint_a = 1.875
quint_b = -1.25
quint_c = 0.375
highest = lax.Precision.HIGH


def row_gram(row_part, whole_part):
    return lax.dot_general(
        row_part, whole_part, (((1,), (1,)), ((), ())), preferred_element_type=jnp.float32
    )


def scatter_sum(x, axis):
    count = lax.axis_size(axis)
    chunks = x.reshape((count, x.shape[0] // count) + x.shape[1:])
    return jnp.sum(lax.all_to_all(chunks, axis, 0, 0, tiled=False), axis=0)


def gather_rows(x, axis):
    count = lax.axis_size(axis)
    return lax.all_to_all(jnp.broadcast_to(x[None], (count,) + x.shape), axis, 0, 0, tiled=False)


def per_device(micro_grads, master, moment, second, left_basis, right_basis, left_stat, right_stat):
    dp_count = lax.axis_size("dp")
    micro_count = micro_grads.shape[1]
    local_sum = jnp.sum(micro_grads[0], axis=0, dtype=jnp.float32)
    grad_piece = scatter_sum(local_sum, "dp") / (micro_count * dp_count)
    new_moment = beta_one * moment + (1.0 - beta_one) * grad_piece
    pieces = gather_rows(jnp.stack([grad_piece, moment]), "dp")
    pieces = jnp.swapaxes(pieces, 0, 1).reshape(2, -1, pieces.shape[-1])
    left_flat = left_basis.T.astype(jnp.bfloat16).reshape(1, -1)
    left_cols = lax.all_to_all(
        jnp.broadcast_to(left_flat, (lax.axis_size("dp"), left_flat.shape[1])), "dp", 0, 0, tiled=False
    )
    left_full = left_cols.reshape(-1, left_basis.shape[0]).T
    moment_left = lax.dot_general(
        left_basis, pieces[1], (((0,), (0,)), ((), ())), precision=highest
    )
    packed = jnp.concatenate([pieces[0], moment_left], axis=0)
    right_full = lax.all_gather(right_basis, "mp", axis=1, tiled=True)
    packed, right_full = lax.optimization_barrier((packed, right_full))
    gathered = lax.all_gather(packed, "mp", axis=1, tiled=True)
    grad_full = gathered[: pieces.shape[1]]
    grad_full, left_full = lax.optimization_barrier((grad_full, left_full))
    moment_turned = jnp.dot(gathered[pieces.shape[1] :], right_basis, precision=highest)

    def rotate(matrix):
        left_part = lax.dot_general(left_basis, matrix, (((0,), (0,)), ((), ())), precision=highest)
        return jnp.dot(left_part, right_basis, precision=highest)

    rot_grad = rotate(grad_full)
    rot_moment = beta_one * moment_turned + (1.0 - beta_one) * rot_grad
    new_second = beta_two * second + (1.0 - beta_two) * rot_grad * rot_grad
    rot_step = rot_moment / (jnp.sqrt(new_second) + adam_eps)
    band_width = right_basis.shape[1]
    band_start = lax.axis_index("mp") * band_width
    grad_band = lax.dynamic_slice_in_dim(grad_full, band_start, band_width, 0)
    grad_strip = lax.dynamic_slice_in_dim(grad_full, band_start, band_width, 1)
    left_outer = lax.dot_general(grad_band, grad_full, (((1,), (1,)), ((), ())), precision=highest)
    right_outer = lax.dot_general(
        grad_strip, grad_full, (((0,), (0,)), ((), ())), precision=highest
    )
    new_left_stat = beta_stat * left_stat + (1.0 - beta_stat) * left_outer
    new_right_stat = beta_stat * right_stat + (1.0 - beta_stat) * right_outer
    order_count = left_stat.shape[1]
    stat_rows = jnp.stack([new_left_stat, new_right_stat]).astype(jnp.bfloat16)
    rot_step, stat_rows = lax.optimization_barrier((rot_step, stat_rows))
    stat_whole = lax.all_gather(stat_rows, "mp", axis=1, tiled=True)
    back_half = scatter_sum(
        lax.dot_general(right_basis, rot_step, (((1,), (1,)), ((), ())), precision=highest),
        "mp",
    )
    step_piece = scatter_sum(
        lax.dot_general(left_basis, back_half, (((1,), (1,)), ((), ())), precision=highest),
        "dp",
    )
    new_master = master - learn_rate * step_piece
    weights_block = gather_rows(new_master.astype(jnp.bfloat16), "dp").reshape(
        -1, new_master.shape[1]
    )
    basis_whole = jnp.stack([left_full.astype(jnp.bfloat16), right_full.astype(jnp.bfloat16)])
    power = jnp.einsum("sij,sjk->sik", stat_whole, basis_whole, preferred_element_type=jnp.float32)
    total = jnp.sum(power * power, axis=(1, 2), keepdims=True)
    start = lax.optimization_barrier(
        (power * lax.rsqrt(total * (4.0 / order_count) + norm_eps)).astype(jnp.bfloat16)
    )
    gram = lax.optimization_barrier(
        jnp.einsum("sij,skj->sik", start, start, preferred_element_type=jnp.float32).astype(
            jnp.bfloat16
        )
    )
    square = jnp.einsum("sij,sjk->sik", gram, gram, preferred_element_type=jnp.float32)
    poly = (quint_b * gram.astype(jnp.float32) + quint_c * square).astype(jnp.bfloat16)
    middle = quint_a * start.astype(jnp.float32) + jnp.einsum(
        "sij,sjk->sik", poly, start, preferred_element_type=jnp.float32
    )
    middle = lax.optimization_barrier(middle.astype(jnp.bfloat16))
    middle_rows = lax.dynamic_slice_in_dim(middle, band_start, band_width, 1)
    gram_two = jnp.einsum(
        "sij,skj->sik", middle_rows, middle, preferred_element_type=jnp.float32
    ).astype(jnp.bfloat16)
    new_bases = 1.5 * middle_rows.astype(jnp.float32) - 0.5 * jnp.einsum(
        "sij,sjk->sik", gram_two, middle, preferred_element_type=jnp.float32
    )
    return (
        weights_block,
        new_master,
        new_moment,
        new_second,
        new_left_stat,
        new_right_stat,
        new_bases[0],
        new_bases[1],
    )


def solution(mesh):
    in_specs = (
        P("dp", None, None, "mp"),
        P("dp", "mp"),
        P("dp", "mp"),
        P("dp", "mp"),
        P(None, "dp"),
        P(None, "mp"),
        P("mp", None),
        P("mp", None),
    )
    out_specs = (
        P(None, "mp"),
        P("dp", "mp"),
        P("dp", "mp"),
        P("dp", "mp"),
        P("mp", None),
        P("mp", None),
        P("mp", None),
        P("mp", None),
    )
    return jax.shard_map(
        per_device, mesh=mesh, in_specs=in_specs, out_specs=out_specs, check_vma=False
    )
```
